256 devices in a mesh: seq: 32 (over x, z), ch: 8 (over y, core).
Axes of the slice: x: 4, y: 4, z: 8, core: 2. Of those that a mesh axis runs over, the one named last changes fastest.
Arguments:
- residual_in: bfloat16 [4096, 32768], P('ch', 'seq'), may hold values from -60 to 60
- key_value: bfloat16 [4096, 32768], P('ch', 'seq'), may hold values from -6 to 6
- query_gate: bfloat16 [4096, 32768], P('ch', 'seq'), may hold values from -6 to 6
- decay_rates: float32 [4096, 16], P('ch'), may hold values from 1 to 1024, as said below
- residues: float32 [4096, 16], P('ch'), may hold values from -1.8 to 1.8
- out_weight: bfloat16 [4096, 4096], P('ch'), may hold values from -0.09375 to 0.09375
- norm_gain: float32 [4096], P('ch'), may hold values from 0.5 to 1.5
Outputs:
- normed_out: bfloat16 [4096, 32768], P('ch', 'seq')
The draws below stay inside these ranges and needn't reach their ends.
Inputs may be any that keep to these rules, and one draw needn't show every extreme that they name: `decay_rates`: each mode's decay over the whole sequence lies between 1 and 1024.
All inputs are finite; a program needn't handle non-finite values.
Results may differ from the reference program's by a relative error of at most 0.017.
Values may be sent and summed in bfloat16 or wider, within the bound.
No kernel may reach another device: no remote copies, remote signals or barrier semaphores. Data moves between devices by JAX's collectives and lax.ppermute only.
A program may use at most 64 MiB of HBM per device.

```python
import math
import jax
import jax.numpy as jnp
from jax import lax

D = 4096
MODES = 16
SEQ_LEN = 32768
N_CH = 8


def draw_decay_rates(key, part):
    lowest = 1.0
    highest_rate = SEQ_LEN / 32.0
    spread = jax.random.uniform(key, (D, MODES), jnp.float32)
    return jnp.exp(jnp.log(lowest) + spread * (jnp.log(highest_rate) - jnp.log(lowest)))


def draw_residual_in(key, part):
    first_key, second_key = jax.random.split(key, 2)
    values = jnp.clip(jax.random.normal(first_key, (D, SEQ_LEN), jnp.float32), -5.5, 5.5)
    channel_exp = jnp.arange(D, dtype=jnp.float32) / D - 0.5
    row_exp = jax.random.uniform(second_key, (1, SEQ_LEN), jnp.float32) - 0.5
    return (values * (10.0 ** channel_exp)[:, None] * 10.0 ** row_exp).astype(jnp.bfloat16)


def level_of(stream_key, extent, cuts, low, largest):
    gain = 1.0
    for axis_at, shards_of in cuts:
        steps = jax.random.uniform(jax.random.fold_in(jax.random.fold_in(stream_key, 6), axis_at), (shards_of,), jnp.float32, low / len(cuts), largest / len(cuts))
        gain = gain * jnp.repeat(jnp.exp(steps), extent[axis_at] // shards_of).reshape((-1,) + (1,) * (len(extent) - 1 - axis_at))
    return gain


def normal_values(rng, shape, scale, reach, cuts=(), held_as=jnp.bfloat16):
    values = scale * jax.random.normal(rng, shape, jnp.float32)
    if cuts:
        values = values * level_of(rng, shape, cuts, -0.22, 0.18)
    return jnp.clip(values, -reach, reach).astype(held_as)


def setup_inputs(seed: int = 0) -> dict:
    keys = jax.random.split(jax.random.key(seed), 8)
    return {
        "residual_in": draw_residual_in(jax.random.fold_in(keys[7], 71), 0),
        "key_value": normal_values(keys[1], (D, SEQ_LEN), 1.0, 6.0, ((0, 8), (1, 32))),
        "query_gate": normal_values(keys[2], (D, SEQ_LEN), 1.0, 6.0, ((0, 8), (1, 32))),
        "decay_rates": draw_decay_rates(jax.random.fold_in(keys[7], 71), 0),
        "residues": normal_values(keys[4], (D, MODES), 0.3, 1.8, ((0, 8),), jnp.float32),
        "out_weight": normal_values(keys[5], (D, D), D ** -0.5, 0.09375, ((0, 8),)),
        "norm_gain": jnp.clip(1.0 + 0.1 * jax.random.normal(keys[6], (D,), jnp.float32), 0.5, 1.5),
    }


highest = lax.Precision.HIGHEST
epsilon = 1e-06

def reference(residual_in, key_value, query_gate, decay_rates, residues, out_weight, norm_gain):
    channels = key_value.shape[0]
    total_len = key_value.shape[1]
    per_group = math.gcd(channels, 64)
    groups = channels // per_group
    shifts = jnp.arange(total_len, dtype=jnp.float32)
    fft_len = 2 * total_len
    rates = decay_rates / total_len

    def filtered(pieces):
        signal, rate_rows, residue_rows = pieces
        weights = residue_rows * jnp.sqrt(2.0 * rate_rows)
        decays = jnp.exp(-rate_rows[:, :, None] * shifts[None, None, :])
        taps = jnp.einsum('gm,gmt->gt', weights, decays, precision=highest)
        spectrum = jnp.fft.rfft(taps, n=fft_len) * jnp.fft.rfft(signal.astype(jnp.float32), n=fft_len)
        return jnp.fft.irfft(spectrum, n=fft_len)[:, :total_len].astype(jnp.float32)
    convolved = lax.map(filtered, (key_value.reshape(groups, per_group, total_len), rates.reshape(groups, per_group, -1), residues.reshape(groups, per_group, -1))).reshape(channels, total_len)
    gated = (query_gate.astype(jnp.float32) * convolved).astype(jnp.bfloat16)
    mixed = residual_in.astype(jnp.float32)
    share = channels // N_CH
    for member in range(N_CH):
        rows = gated[member * share:(member + 1) * share]
        weight_rows = out_weight[member * share:(member + 1) * share]
        partial_sum = jnp.dot(weight_rows.T, rows, preferred_element_type=jnp.float32).astype(jnp.bfloat16)
        mixed = mixed + partial_sum.astype(jnp.float32)
    square_mean = lax.optimization_barrier(jnp.mean(mixed * mixed, axis=0))
    scaled = mixed * lax.rsqrt(square_mean + epsilon)[None, :] * norm_gain[:, None]
    return scaled.astype(jnp.bfloat16)
```

```python
import functools

import jax
import jax.numpy as jnp
from jax import lax
from jax.experimental import pallas as pl
from jax.experimental.pallas import tpu as pltpu
from jax.sharding import PartitionSpec as P

highest = lax.Precision.HIGHEST
epsilon = 1e-06
block_len = 256
tile_ch = 64


def conv_kernel(x_ref, g_ref, p_ref, o_ref):
    modes = p_ref.shape[1]
    tc, seg = x_ref.shape
    L = block_len
    shape = (modes, tc, L)
    rate = jnp.broadcast_to(p_ref[0][:, :, 0:1], shape)
    weight = jnp.broadcast_to(p_ref[1][:, :, 0:1], shape)
    state = jnp.broadcast_to(p_ref[2][:, :, 0:1], shape)
    pos = lax.broadcasted_iota(jnp.int32, shape, 2).astype(jnp.float32)
    grow = jnp.exp(rate * pos)
    shrink = weight * jnp.exp(-rate * pos)
    step_decay = jnp.exp(-rate)
    block_decay = jnp.exp(-rate * (L - 1.0))
    first = pos == 0.0
    rows = lax.broadcasted_iota(jnp.int32, (L, L), 0)
    cols = lax.broadcasted_iota(jnp.int32, (L, L), 1)
    upper = (rows <= cols).astype(jnp.bfloat16)
    for b in range(seg // L):
        xb = x_ref[:, b * L:(b + 1) * L].astype(jnp.float32)
        u = xb[None] * grow + jnp.where(first, step_decay * state, 0.0)
        u2 = u.reshape(modes * tc, L)
        hi = u2.astype(jnp.bfloat16)
        lo = (u2 - hi.astype(jnp.float32)).astype(jnp.bfloat16)
        pre = jnp.dot(hi, upper, preferred_element_type=jnp.float32) + jnp.dot(
            lo, upper, preferred_element_type=jnp.float32
        )
        pre = pre.reshape(modes, tc, L)
        conv = jnp.sum(shrink * pre, axis=0)
        state = jnp.broadcast_to(pre[:, :, L - 1:L], shape) * block_decay
        gate = g_ref[:, b * L:(b + 1) * L].astype(jnp.float32)
        o_ref[:, b * L:(b + 1) * L] = (gate * conv).astype(o_ref.dtype)


def gated_conv(signal, gate, params):
    rows, seg = signal.shape
    modes = params.shape[1]
    tc = tile_ch
    return pl.pallas_call(
        conv_kernel,
        out_shape=jax.ShapeDtypeStruct((rows, seg), jnp.bfloat16),
        grid=(rows // tc,),
        in_specs=[
            pl.BlockSpec((tc, seg), lambda i: (i, 0)),
            pl.BlockSpec((tc, seg), lambda i: (i, 0)),
            pl.BlockSpec((3, modes, tc, 128), lambda i: (0, 0, i, 0)),
        ],
        out_specs=pl.BlockSpec((tc, seg), lambda i: (i, 0)),
        compiler_params=pltpu.CompilerParams(vmem_limit_bytes=48 * 1024 * 1024),
        cost_estimate=pl.CostEstimate(
            flops=4 * rows * seg * modes * block_len + 12 * rows * seg * modes,
            transcendentals=2 * rows * modes * block_len,
            bytes_accessed=6 * rows * seg + 3 * modes * rows * 128 * 4,
        ),
    )(signal, gate, params)


def local_end_state(signal, rates):
    rows, seg = signal.shape
    L = block_len
    nb = seg // L
    pos = jnp.arange(L, dtype=jnp.float32)
    blocks = signal.astype(jnp.float32).reshape(rows, nb, L)
    tail = jnp.exp(-rates[:, :, None] * (L - 1.0 - pos)[None, None, :])
    per_block = jnp.einsum("cbs,cms->cbm", blocks, tail, precision=highest)
    later = (nb - 1.0 - jnp.arange(nb, dtype=jnp.float32)) * L
    carry = jnp.exp(-rates[:, None, :] * later[None, :, None])
    return jnp.sum(per_block * carry, axis=1)


def per_device(residual_in, key_value, query_gate, decay_rates, residues, out_weight, norm_gain):
    rows, seg_len = key_value.shape
    n_seq = lax.axis_size("seq")
    total_len = n_seq * seg_len
    rates = decay_rates / total_len
    weights = residues * jnp.sqrt(2.0 * rates)
    own_end = local_end_state(key_value, rates)
    ends = lax.all_gather(own_end, "seq")
    me = lax.axis_index("seq")
    others = jnp.arange(n_seq)
    gap = jnp.maximum(me - 1 - others, 0).astype(jnp.float32) * seg_len
    span = jnp.where(
        (others < me)[:, None, None],
        jnp.exp(-rates[None] * gap[:, None, None]),
        0.0,
    )
    carry_in = jnp.sum(span * ends, axis=0)
    packed = jnp.stack([rates.T, weights.T, carry_in.T])
    packed = jnp.broadcast_to(packed[..., None], packed.shape + (128,))
    gated = gated_conv(key_value, query_gate, packed)
    summed = lax.psum_scatter(
        lax.dot_general(
            out_weight, gated, (((0,), (0,)), ((), ())), preferred_element_type=jnp.float32
        ).astype(jnp.bfloat16),
        "ch",
        scatter_dimension=0,
        tiled=True,
    ).astype(jnp.float32)
    mixed = residual_in.astype(jnp.float32) + summed
    squares = lax.psum(jnp.sum(mixed * mixed, axis=0), "ch")
    square_mean = squares / out_weight.shape[1]
    scaled = mixed * lax.rsqrt(square_mean + epsilon)[None, :] * norm_gain[:, None]
    return scaled.astype(jnp.bfloat16)


def solution(mesh):
    placed = (
        P("ch", "seq"),
        P("ch", "seq"),
        P("ch", "seq"),
        P("ch", None),
        P("ch", None),
        P("ch", None),
        P("ch"),
    )
    return jax.shard_map(
        per_device, mesh=mesh, in_specs=placed, out_specs=P("ch", "seq"), check_vma=False
    )
```

```python
import functools

import jax
import jax.numpy as jnp
from jax import lax
from jax.experimental import pallas as pl
from jax.experimental.pallas import tpu as pltpu
from jax.sharding import PartitionSpec as P

highest = lax.Precision.HIGHEST
epsilon = 1e-06
block_len = 256
tile_ch = 64


def conv_kernel(x_ref, g_ref, p_ref, o_ref):
    modes = p_ref.shape[0]
    tc, seg = x_ref.shape
    L = block_len
    shape = (modes, tc, L)
    p = p_ref[...]
    half = (modes, tc, 128)
    rate_h = jnp.broadcast_to(p[:, :, 0:1], half)
    step_h = jnp.exp(-rate_h)
    end_h = jnp.exp(-rate_h * (L - 1.0))
    rate = jnp.concatenate([rate_h, rate_h], axis=2)
    weight = jnp.broadcast_to(p[:, :, 1:2], shape)
    state = jnp.broadcast_to(p[:, :, 2:3], shape)
    pos = lax.broadcasted_iota(jnp.int32, shape, 2).astype(jnp.float32)
    grow = jnp.exp(rate * pos)
    shrink = weight * jnp.exp(-rate * pos)
    step_decay = jnp.concatenate([step_h, step_h], axis=2)
    block_decay = jnp.concatenate([end_h, end_h], axis=2)
    first = pos == 0.0
    rows = lax.broadcasted_iota(jnp.int32, (L, L), 0)
    cols = lax.broadcasted_iota(jnp.int32, (L, L), 1)
    upper = (rows <= cols).astype(jnp.bfloat16)
    for b in range(seg // L):
        xb = x_ref[:, b * L:(b + 1) * L].astype(jnp.float32)
        u = xb[None] * grow + jnp.where(first, step_decay * state, 0.0)
        u2 = u.reshape(modes * tc, L)
        hi = u2.astype(jnp.bfloat16)
        lo = (u2 - hi.astype(jnp.float32)).astype(jnp.bfloat16)
        pre = jnp.dot(hi, upper, preferred_element_type=jnp.float32) + jnp.dot(
            lo, upper, preferred_element_type=jnp.float32
        )
        pre = pre.reshape(modes, tc, L)
        conv = jnp.sum(shrink * pre, axis=0)
        state = jnp.broadcast_to(pre[:, :, L - 1:L], shape) * block_decay
        gate = g_ref[:, b * L:(b + 1) * L].astype(jnp.float32)
        o_ref[:, b * L:(b + 1) * L] = (gate * conv).astype(o_ref.dtype)


def gated_conv(signal, gate, params):
    rows, seg = signal.shape
    modes = params.shape[0]
    tc = tile_ch
    return pl.pallas_call(
        conv_kernel,
        out_shape=jax.ShapeDtypeStruct((rows, seg), jnp.bfloat16),
        grid=(rows // tc,),
        in_specs=[
            pl.BlockSpec((tc, seg), lambda i: (i, 0)),
            pl.BlockSpec((tc, seg), lambda i: (i, 0)),
            pl.BlockSpec((modes, tc, 128), lambda i: (0, i, 0)),
        ],
        out_specs=pl.BlockSpec((tc, seg), lambda i: (i, 0)),
        compiler_params=pltpu.CompilerParams(vmem_limit_bytes=48 * 1024 * 1024),
        cost_estimate=pl.CostEstimate(
            flops=4 * rows * seg * modes * block_len + 12 * rows * seg * modes,
            transcendentals=2 * rows * modes * block_len,
            bytes_accessed=6 * rows * seg + modes * rows * 128 * 4,
        ),
    )(signal, gate, params)


def end_kernel(x_ref, p_ref, o_ref):
    modes = p_ref.shape[0]
    tc, seg = x_ref.shape
    L = block_len
    nb = seg // L
    shape = (modes, tc, L)
    rate = jnp.broadcast_to(p_ref[...][:, :, 0:1], shape)
    pos = lax.broadcasted_iota(jnp.int32, shape, 2).astype(jnp.float32)
    tail = jnp.exp(-rate * (L - 1.0 - pos))
    whole = jnp.exp(-rate * float(L))
    total = jnp.zeros(shape, jnp.float32)
    for b in range(nb):
        xb = x_ref[:, b * L:(b + 1) * L].astype(jnp.float32)
        total = total * whole + xb[None] * tail
    summed = jnp.sum(total, axis=2, keepdims=True)
    o_ref[...] = jnp.broadcast_to(summed, (modes, tc, 128))


def local_end_state(signal, params):
    rows, seg = signal.shape
    modes = params.shape[0]
    tc = tile_ch
    return pl.pallas_call(
        end_kernel,
        out_shape=jax.ShapeDtypeStruct((modes, rows, 128), jnp.float32),
        grid=(rows // tc,),
        in_specs=[
            pl.BlockSpec((tc, seg), lambda i: (i, 0)),
            pl.BlockSpec((modes, tc, 128), lambda i: (0, i, 0)),
        ],
        out_specs=pl.BlockSpec((modes, tc, 128), lambda i: (0, i, 0)),
        compiler_params=pltpu.CompilerParams(vmem_limit_bytes=48 * 1024 * 1024),
        cost_estimate=pl.CostEstimate(
            flops=3 * rows * seg * modes,
            transcendentals=rows * seg * modes,
            bytes_accessed=2 * rows * seg + 2 * modes * rows * 128 * 4,
        ),
    )(signal, params)[:, :, 0]


def per_device(residual_in, key_value, query_gate, decay_rates, residues, out_weight, norm_gain):
    rows, seg_len = key_value.shape
    n_seq = lax.axis_size("seq")
    total_len = n_seq * seg_len
    rates = decay_rates / total_len
    weights = residues * jnp.sqrt(2.0 * rates)
    lanes = lax.broadcasted_iota(jnp.int32, (1, 1, 128), 2)
    base = jnp.where(lanes == 0, rates.T[:, :, None], 0.0) + jnp.where(
        lanes == 1, weights.T[:, :, None], 0.0
    )
    own_end = local_end_state(key_value, base)
    block_decay = jnp.exp(-rates.T * seg_len)
    carry_in = lax.ppermute(own_end, "seq", [(i, i + 1) for i in range(n_seq - 1)])
    shift = 1
    factor = block_decay
    while shift < n_seq:
        moved = lax.ppermute(carry_in, "seq", [(i, i + shift) for i in range(n_seq - shift)])
        carry_in = carry_in + factor * moved
        factor = factor * factor
        shift *= 2
    packed = base + jnp.where(lanes == 2, carry_in[:, :, None], 0.0)
    gated = gated_conv(key_value, query_gate, packed)
    summed = lax.psum_scatter(
        lax.dot_general(
            out_weight, gated, (((0,), (0,)), ((), ())), preferred_element_type=jnp.float32
        ).astype(jnp.bfloat16),
        "ch",
        scatter_dimension=0,
        tiled=True,
    ).astype(jnp.float32)
    mixed = residual_in.astype(jnp.float32) + summed
    squares = lax.psum(jnp.sum(mixed * mixed, axis=0), "ch")
    square_mean = squares / out_weight.shape[1]
    scaled = mixed * lax.rsqrt(square_mean + epsilon)[None, :] * norm_gain[:, None]
    return scaled.astype(jnp.bfloat16)


def solution(mesh):
    placed = (
        P("ch", "seq"),
        P("ch", "seq"),
        P("ch", "seq"),
        P("ch", None),
        P("ch", None),
        P("ch", None),
        P("ch"),
    )
    return jax.shard_map(
        per_device, mesh=mesh, in_specs=placed, out_specs=P("ch", "seq"), check_vma=False
    )
```

```python
import functools

import jax
import jax.numpy as jnp
from jax import lax
from jax.experimental import pallas as pl
from jax.experimental.pallas import tpu as pltpu
from jax.sharding import PartitionSpec as P

highest = lax.Precision.HIGHEST
epsilon = 1e-06
block_len = 256
tile_ch = 64


def conv_kernel(x_ref, g_ref, p_ref, o_ref):
    modes = p_ref.shape[0]
    tc, seg = x_ref.shape
    L = block_len
    shape = (modes, tc, L)
    p = p_ref[...]
    half = (modes, tc, 128)
    rate_h = jnp.broadcast_to(p[:, :, 0:1], half)
    step_h = jnp.exp(-rate_h)
    end_h = jnp.exp(-rate_h * (L - 1.0))
    rate = jnp.concatenate([rate_h, rate_h], axis=2)
    weight = jnp.broadcast_to(p[:, :, 1:2], shape)
    state = jnp.broadcast_to(p[:, :, 2:3], shape)
    pos = lax.broadcasted_iota(jnp.int32, shape, 2).astype(jnp.float32)
    grow = jnp.exp(rate * pos)
    shrink = weight * jnp.exp(-rate * pos)
    step_decay = jnp.concatenate([step_h, step_h], axis=2)
    block_decay = jnp.concatenate([end_h, end_h], axis=2)
    first = pos == 0.0
    rows = lax.broadcasted_iota(jnp.int32, (L, L), 0)
    cols = lax.broadcasted_iota(jnp.int32, (L, L), 1)
    upper = (rows <= cols).astype(jnp.bfloat16)
    for b in range(seg // L):
        xb = x_ref[:, b * L:(b + 1) * L].astype(jnp.float32)
        u = xb[None] * grow + jnp.where(first, step_decay * state, 0.0)
        u2 = u.reshape(modes * tc, L)
        hi = u2.astype(jnp.bfloat16)
        lo = (u2 - hi.astype(jnp.float32)).astype(jnp.bfloat16)
        pre = jnp.dot(hi, upper, preferred_element_type=jnp.float32) + jnp.dot(
            lo, upper, preferred_element_type=jnp.float32
        )
        pre = pre.reshape(modes, tc, L)
        conv = jnp.sum(shrink * pre, axis=0)
        state = jnp.broadcast_to(pre[:, :, L - 1:L], shape) * block_decay
        gate = g_ref[:, b * L:(b + 1) * L].astype(jnp.float32)
        o_ref[:, b * L:(b + 1) * L] = (gate * conv).astype(o_ref.dtype)


def gated_conv(signal, gate, params):
    rows, seg = signal.shape
    modes = params.shape[0]
    tc = tile_ch
    return pl.pallas_call(
        conv_kernel,
        out_shape=jax.ShapeDtypeStruct((rows, seg), jnp.bfloat16),
        grid=(rows // tc,),
        in_specs=[
            pl.BlockSpec((tc, seg), lambda i: (i, 0)),
            pl.BlockSpec((tc, seg), lambda i: (i, 0)),
            pl.BlockSpec((modes, tc, 128), lambda i: (0, i, 0)),
        ],
        out_specs=pl.BlockSpec((tc, seg), lambda i: (i, 0)),
        compiler_params=pltpu.CompilerParams(vmem_limit_bytes=48 * 1024 * 1024),
        cost_estimate=pl.CostEstimate(
            flops=4 * rows * seg * modes * block_len + 12 * rows * seg * modes,
            transcendentals=2 * rows * modes * block_len,
            bytes_accessed=6 * rows * seg + modes * rows * 128 * 4,
        ),
    )(signal, gate, params)


def end_kernel(x_ref, p_ref, o_ref):
    modes = p_ref.shape[0]
    tc, seg = x_ref.shape
    L = block_len
    nb = seg // L
    shape = (modes, tc, L)
    rate = jnp.broadcast_to(p_ref[...][:, :, 0:1], shape)
    pos = lax.broadcasted_iota(jnp.int32, shape, 2).astype(jnp.float32)
    tail = jnp.exp(-rate * (L - 1.0 - pos))
    whole = jnp.exp(-rate * float(L))
    total = jnp.zeros(shape, jnp.float32)
    for b in range(nb):
        xb = x_ref[:, b * L:(b + 1) * L].astype(jnp.float32)
        total = total * whole + xb[None] * tail
    summed = jnp.sum(total, axis=2, keepdims=True)
    o_ref[...] = jnp.broadcast_to(summed, (modes, tc, 128))


def local_end_state(signal, params):
    rows, seg = signal.shape
    modes = params.shape[0]
    tc = tile_ch
    return pl.pallas_call(
        end_kernel,
        out_shape=jax.ShapeDtypeStruct((modes, rows, 128), jnp.float32),
        grid=(rows // tc,),
        in_specs=[
            pl.BlockSpec((tc, seg), lambda i: (i, 0)),
            pl.BlockSpec((modes, tc, 128), lambda i: (0, i, 0)),
        ],
        out_specs=pl.BlockSpec((modes, tc, 128), lambda i: (0, i, 0)),
        compiler_params=pltpu.CompilerParams(vmem_limit_bytes=48 * 1024 * 1024),
        cost_estimate=pl.CostEstimate(
            flops=3 * rows * seg * modes,
            transcendentals=rows * seg * modes,
            bytes_accessed=2 * rows * seg + 2 * modes * rows * 128 * 4,
        ),
    )(signal, params)[:, :, 0]


def per_device(residual_in, key_value, query_gate, decay_rates, residues, out_weight, norm_gain):
    rows, seg_len = key_value.shape
    n_seq = lax.axis_size("seq")
    total_len = n_seq * seg_len
    rates = decay_rates / total_len
    weights = residues * jnp.sqrt(2.0 * rates)
    lanes = lax.broadcasted_iota(jnp.int32, (1, 1, 128), 2)
    base = jnp.where(lanes == 0, rates.T[:, :, None], 0.0) + jnp.where(
        lanes == 1, weights.T[:, :, None], 0.0
    )
    own_end = local_end_state(key_value, base)
    block_decay = jnp.exp(-rates.T * seg_len)
    carry_in = jnp.zeros_like(own_end)
    factor = jnp.ones_like(block_decay)
    for shift in range(1, n_seq):
        moved = lax.ppermute(own_end, "seq", [(i, i + shift) for i in range(n_seq - shift)])
        carry_in = carry_in + factor * moved
        factor = factor * block_decay
    packed = base + jnp.where(lanes == 2, carry_in[:, :, None], 0.0)
    gated = gated_conv(key_value, query_gate, packed)
    summed = lax.psum_scatter(
        lax.dot_general(
            out_weight, gated, (((0,), (0,)), ((), ())), preferred_element_type=jnp.float32
        ).astype(jnp.bfloat16),
        "ch",
        scatter_dimension=0,
        tiled=True,
    ).astype(jnp.float32)
    mixed = residual_in.astype(jnp.float32) + summed
    squares = lax.psum(jnp.sum(mixed * mixed, axis=0), "ch")
    square_mean = squares / out_weight.shape[1]
    scaled = mixed * lax.rsqrt(square_mean + epsilon)[None, :] * norm_gain[:, None]
    return scaled.astype(jnp.bfloat16)


def solution(mesh):
    placed = (
        P("ch", "seq"),
        P("ch", "seq"),
        P("ch", "seq"),
        P("ch", None),
        P("ch", None),
        P("ch", None),
        P("ch"),
    )
    return jax.shard_map(
        per_device, mesh=mesh, in_specs=placed, out_specs=P("ch", "seq"), check_vma=False
    )
```

```python
import functools

import jax
import jax.numpy as jnp
from jax import lax
from jax.experimental import pallas as pl
from jax.experimental.pallas import tpu as pltpu
from jax.sharding import PartitionSpec as P

highest = lax.Precision.HIGHEST
epsilon = 1e-06
block_len = 256
tile_ch = 64


def conv_kernel(x_ref, g_ref, p_ref, o_ref):
    modes = p_ref.shape[0]
    tc, seg = x_ref.shape
    L = block_len
    shape = (modes, tc, L)
    p = p_ref[...]
    half = (modes, tc, 128)
    rate_h = jnp.broadcast_to(p[:, :, 0:1], half)
    step_h = jnp.exp(-rate_h)
    end_h = jnp.exp(-rate_h * (L - 1.0))
    rate = jnp.concatenate([rate_h, rate_h], axis=2)
    weight = jnp.broadcast_to(p[:, :, 1:2], shape)
    state = jnp.broadcast_to(p[:, :, 2:3], shape)
    pos = lax.broadcasted_iota(jnp.int32, shape, 2).astype(jnp.float32)
    grow = jnp.exp(rate * pos)
    shrink = weight * jnp.exp(-rate * pos)
    step_decay = jnp.concatenate([step_h, step_h], axis=2)
    block_decay = jnp.concatenate([end_h, end_h], axis=2)
    first = pos == 0.0
    rows = lax.broadcasted_iota(jnp.int32, (L, L), 0)
    cols = lax.broadcasted_iota(jnp.int32, (L, L), 1)
    upper = (rows <= cols).astype(jnp.bfloat16)
    for b in range(seg // L):
        xb = x_ref[:, b * L:(b + 1) * L].astype(jnp.float32)
        u = xb[None] * grow + jnp.where(first, step_decay * state, 0.0)
        u2 = u.reshape(modes * tc, L)
        hi = u2.astype(jnp.bfloat16)
        lo = (u2 - hi.astype(jnp.float32)).astype(jnp.bfloat16)
        pre = jnp.dot(hi, upper, preferred_element_type=jnp.float32) + jnp.dot(
            lo, upper, preferred_element_type=jnp.float32
        )
        pre = pre.reshape(modes, tc, L)
        conv = jnp.sum(shrink * pre, axis=0)
        state = jnp.broadcast_to(pre[:, :, L - 1:L], shape) * block_decay
        gate = g_ref[:, b * L:(b + 1) * L].astype(jnp.float32)
        o_ref[:, b * L:(b + 1) * L] = (gate * conv).astype(o_ref.dtype)


def gated_conv(signal, gate, params):
    rows, seg = signal.shape
    modes = params.shape[0]
    tc = tile_ch
    return pl.pallas_call(
        conv_kernel,
        out_shape=jax.ShapeDtypeStruct((rows, seg), jnp.bfloat16),
        grid=(rows // tc,),
        in_specs=[
            pl.BlockSpec((tc, seg), lambda i: (i, 0)),
            pl.BlockSpec((tc, seg), lambda i: (i, 0)),
            pl.BlockSpec((modes, tc, 128), lambda i: (0, i, 0)),
        ],
        out_specs=pl.BlockSpec((tc, seg), lambda i: (i, 0)),
        compiler_params=pltpu.CompilerParams(vmem_limit_bytes=48 * 1024 * 1024),
        cost_estimate=pl.CostEstimate(
            flops=4 * rows * seg * modes * block_len + 12 * rows * seg * modes,
            transcendentals=2 * rows * modes * block_len,
            bytes_accessed=6 * rows * seg + modes * rows * 128 * 4,
        ),
    )(signal, gate, params)


def end_kernel(x_ref, p_ref, o_ref):
    modes = p_ref.shape[0]
    tc, seg = x_ref.shape
    L = block_len
    nb = seg // L
    shape = (modes, tc, L)
    rate = jnp.broadcast_to(p_ref[...][:, :, 0:1], shape)
    pos = lax.broadcasted_iota(jnp.int32, shape, 2).astype(jnp.float32)
    tail = jnp.exp(-rate * (L - 1.0 - pos))
    whole = jnp.exp(-rate * float(L))
    total = jnp.zeros(shape, jnp.float32)
    for b in range(nb):
        xb = x_ref[:, b * L:(b + 1) * L].astype(jnp.float32)
        total = total * whole + xb[None] * tail
    summed = jnp.sum(total, axis=2, keepdims=True)
    o_ref[...] = jnp.broadcast_to(summed, (modes, tc, 128))


def local_end_state(signal, params):
    rows, seg = signal.shape
    modes = params.shape[0]
    tc = tile_ch
    return pl.pallas_call(
        end_kernel,
        out_shape=jax.ShapeDtypeStruct((modes, rows, 128), jnp.float32),
        grid=(rows // tc,),
        in_specs=[
            pl.BlockSpec((tc, seg), lambda i: (i, 0)),
            pl.BlockSpec((modes, tc, 128), lambda i: (0, i, 0)),
        ],
        out_specs=pl.BlockSpec((modes, tc, 128), lambda i: (0, i, 0)),
        compiler_params=pltpu.CompilerParams(vmem_limit_bytes=48 * 1024 * 1024),
        cost_estimate=pl.CostEstimate(
            flops=3 * rows * seg * modes,
            transcendentals=rows * seg * modes,
            bytes_accessed=2 * rows * seg + 2 * modes * rows * 128 * 4,
        ),
    )(signal, params)[:, :, 0]


def per_device(residual_in, key_value, query_gate, decay_rates, residues, out_weight, norm_gain):
    rows, seg_len = key_value.shape
    n_seq = lax.axis_size("seq")
    total_len = n_seq * seg_len
    rates = decay_rates / total_len
    weights = residues * jnp.sqrt(2.0 * rates)
    lanes = lax.broadcasted_iota(jnp.int32, (1, 1, 128), 2)
    base = jnp.where(lanes == 0, rates.T[:, :, None], 0.0) + jnp.where(
        lanes == 1, weights.T[:, :, None], 0.0
    )
    own_end = local_end_state(key_value, base)
    block_decay = jnp.exp(-rates.T * seg_len)

    def shifted(value, shift):
        return lax.ppermute(value, "seq", [(i, i + shift) for i in range(n_seq - shift)])

    carry_in = jnp.zeros_like(own_end)
    factor = jnp.ones_like(block_decay)
    for shift in range(1, 5):
        carry_in = carry_in + factor * shifted(own_end, shift)
        factor = factor * block_decay
    span = 4
    while span < n_seq:
        step = factor
        window = carry_in
        for q in range(1, 4):
            if q * span >= n_seq:
                break
            carry_in = carry_in + factor * shifted(window, q * span)
            factor = factor * step
        span *= 4
    packed = base + jnp.where(lanes == 2, carry_in[:, :, None], 0.0)
    gated = gated_conv(key_value, query_gate, packed)
    summed = lax.psum_scatter(
        lax.dot_general(
            out_weight, gated, (((0,), (0,)), ((), ())), preferred_element_type=jnp.float32
        ).astype(jnp.bfloat16),
        "ch",
        scatter_dimension=0,
        tiled=True,
    ).astype(jnp.float32)
    mixed = residual_in.astype(jnp.float32) + summed
    squares = lax.psum(jnp.sum(mixed * mixed, axis=0), "ch")
    square_mean = squares / out_weight.shape[1]
    scaled = mixed * lax.rsqrt(square_mean + epsilon)[None, :] * norm_gain[:, None]
    return scaled.astype(jnp.bfloat16)


def solution(mesh):
    placed = (
        P("ch", "seq"),
        P("ch", "seq"),
        P("ch", "seq"),
        P("ch", None),
        P("ch", None),
        P("ch", None),
        P("ch"),
    )
    return jax.shard_map(
        per_device, mesh=mesh, in_specs=placed, out_specs=P("ch", "seq"), check_vma=False
    )
```

```python
import functools

import jax
import jax.numpy as jnp
from jax import lax
from jax.experimental import pallas as pl
from jax.experimental.pallas import tpu as pltpu
from jax.sharding import PartitionSpec as P

highest = lax.Precision.HIGHEST
epsilon = 1e-06
block_len = 256
tile_ch = 64


def conv_kernel(x_ref, g_ref, p_ref, o_ref, n_ref):
    modes = p_ref.shape[0]
    tc, L = x_ref.shape
    shape = (modes, tc, L)
    p = p_ref[...]
    half = (modes, tc, 128)
    rate_h = jnp.broadcast_to(p[:, :, 0:1], half)
    step_h = jnp.exp(-rate_h)
    end_h = jnp.exp(-rate_h * (L - 1.0))
    rate = jnp.concatenate([rate_h] * (L // 128), axis=2)
    step_decay = jnp.concatenate([step_h] * (L // 128), axis=2)
    weight = jnp.broadcast_to(p[:, :, 1:2], shape)
    state = jnp.broadcast_to(p[:, :, 2:3], shape)
    pos = lax.broadcasted_iota(jnp.int32, shape, 2).astype(jnp.float32)
    grow = jnp.exp(rate * pos)
    shrink = weight * jnp.exp(-rate * pos)
    rows = lax.broadcasted_iota(jnp.int32, (L, L), 0)
    cols = lax.broadcasted_iota(jnp.int32, (L, L), 1)
    upper = (rows <= cols).astype(jnp.bfloat16)
    xb = x_ref[...].astype(jnp.float32)
    u = xb[None] * grow + jnp.where(pos == 0.0, step_decay * state, 0.0)
    u2 = u.reshape(modes * tc, L)
    hi = u2.astype(jnp.bfloat16)
    lo = (u2 - hi.astype(jnp.float32)).astype(jnp.bfloat16)
    pre = jnp.dot(hi, upper, preferred_element_type=jnp.float32) + jnp.dot(
        lo, upper, preferred_element_type=jnp.float32
    )
    pre = pre.reshape(modes, tc, L)
    conv = jnp.sum(shrink * pre, axis=0)
    o_ref[...] = (g_ref[...].astype(jnp.float32) * conv).astype(o_ref.dtype)
    after = jnp.broadcast_to(pre[:, :, L - 1:L], half) * end_h
    lanes = lax.broadcasted_iota(jnp.int32, half, 2)
    n_ref[...] = jnp.where(lanes == 2, after, p)


def gated_conv_block(signal, gate, params, b):
    rows, seg = signal.shape
    modes = params.shape[0]
    tc = tile_ch
    L = block_len
    return pl.pallas_call(
        conv_kernel,
        out_shape=(
            jax.ShapeDtypeStruct((rows, L), jnp.bfloat16),
            jax.ShapeDtypeStruct(params.shape, jnp.float32),
        ),
        grid=(rows // tc,),
        in_specs=[
            pl.BlockSpec((tc, L), lambda i: (i, b)),
            pl.BlockSpec((tc, L), lambda i: (i, b)),
            pl.BlockSpec((modes, tc, 128), lambda i: (0, i, 0)),
        ],
        out_specs=(
            pl.BlockSpec((tc, L), lambda i: (i, 0)),
            pl.BlockSpec((modes, tc, 128), lambda i: (0, i, 0)),
        ),
        compiler_params=pltpu.CompilerParams(vmem_limit_bytes=48 * 1024 * 1024),
        cost_estimate=pl.CostEstimate(
            flops=4 * rows * L * modes * L + 12 * rows * L * modes,
            transcendentals=2 * rows * modes * L,
            bytes_accessed=6 * rows * L + 2 * modes * rows * 128 * 4,
        ),
    )(signal, gate, params)


def end_kernel(x_ref, p_ref, o_ref):
    modes = p_ref.shape[0]
    tc, seg = x_ref.shape
    L = block_len
    nb = seg // L
    shape = (modes, tc, L)
    rate = jnp.broadcast_to(p_ref[...][:, :, 0:1], shape)
    pos = lax.broadcasted_iota(jnp.int32, shape, 2).astype(jnp.float32)
    tail = jnp.exp(-rate * (L - 1.0 - pos))
    whole = jnp.exp(-rate * float(L))
    total = jnp.zeros(shape, jnp.float32)
    for b in range(nb):
        xb = x_ref[:, b * L:(b + 1) * L].astype(jnp.float32)
        total = total * whole + xb[None] * tail
    summed = jnp.sum(total, axis=2, keepdims=True)
    o_ref[...] = jnp.broadcast_to(summed, (modes, tc, 128))


def local_end_state(signal, params):
    rows, seg = signal.shape
    modes = params.shape[0]
    tc = tile_ch
    return pl.pallas_call(
        end_kernel,
        out_shape=jax.ShapeDtypeStruct((modes, rows, 128), jnp.float32),
        grid=(rows // tc,),
        in_specs=[
            pl.BlockSpec((tc, seg), lambda i: (i, 0)),
            pl.BlockSpec((modes, tc, 128), lambda i: (0, i, 0)),
        ],
        out_specs=pl.BlockSpec((modes, tc, 128), lambda i: (0, i, 0)),
        compiler_params=pltpu.CompilerParams(vmem_limit_bytes=48 * 1024 * 1024),
        cost_estimate=pl.CostEstimate(
            flops=3 * rows * seg * modes,
            transcendentals=rows * seg * modes,
            bytes_accessed=2 * rows * seg + 2 * modes * rows * 128 * 4,
        ),
    )(signal, params)[:, :, 0]


def per_device(residual_in, key_value, query_gate, decay_rates, residues, out_weight, norm_gain):
    rows, seg_len = key_value.shape
    n_seq = lax.axis_size("seq")
    total_len = n_seq * seg_len
    rates = decay_rates / total_len
    weights = residues * jnp.sqrt(2.0 * rates)
    lanes = lax.broadcasted_iota(jnp.int32, (1, 1, 128), 2)
    base = jnp.where(lanes == 0, rates.T[:, :, None], 0.0) + jnp.where(
        lanes == 1, weights.T[:, :, None], 0.0
    )
    own_end = local_end_state(key_value, base)
    block_decay = jnp.exp(-rates.T * seg_len)

    def shifted(value, shift):
        return lax.ppermute(value, "seq", [(i, i + shift) for i in range(n_seq - shift)])

    carry_in = jnp.zeros_like(own_end)
    factor = jnp.ones_like(block_decay)
    for shift in range(1, 5):
        carry_in = carry_in + factor * shifted(own_end, shift)
        factor = factor * block_decay
    span = 4
    while span < n_seq:
        step = factor
        window = carry_in
        for q in range(1, 4):
            if q * span >= n_seq:
                break
            carry_in = carry_in + factor * shifted(window, q * span)
            factor = factor * step
        span *= 4
    packed = base + jnp.where(lanes == 2, carry_in[:, :, None], 0.0)
    mixed_parts = []
    for b in range(seg_len // block_len):
        gated, packed = gated_conv_block(key_value, query_gate, packed, b)
        part = lax.dot_general(
            out_weight, gated, (((0,), (0,)), ((), ())), preferred_element_type=jnp.float32
        ).astype(jnp.bfloat16)
        part, packed = lax.optimization_barrier((part, packed))
        summed = lax.psum_scatter(
            part,
            "ch",
            scatter_dimension=0,
            tiled=True,
        ).astype(jnp.float32)
        here = residual_in[:, b * block_len:(b + 1) * block_len].astype(jnp.float32)
        mixed_parts.append(here + summed)
    mixed = jnp.concatenate(mixed_parts, axis=1)
    squares = lax.psum(jnp.sum(mixed * mixed, axis=0), "ch")
    square_mean = squares / out_weight.shape[1]
    scaled = mixed * lax.rsqrt(square_mean + epsilon)[None, :] * norm_gain[:, None]
    return scaled.astype(jnp.bfloat16)


def solution(mesh):
    placed = (
        P("ch", "seq"),
        P("ch", "seq"),
        P("ch", "seq"),
        P("ch", None),
        P("ch", None),
        P("ch", None),
        P("ch"),
    )
    return jax.shard_map(
        per_device, mesh=mesh, in_specs=placed, out_specs=P("ch", "seq"), check_vma=False
    )
```

```python
import functools

import jax
import jax.numpy as jnp
from jax import lax
from jax.experimental import pallas as pl
from jax.experimental.pallas import tpu as pltpu
from jax.sharding import PartitionSpec as P

highest = lax.Precision.HIGHEST
epsilon = 1e-06
block_len = 256
tile_ch = 128


def expand(v, length):
    modes, tc = v.shape
    vt = v.T
    return jnp.stack([jnp.broadcast_to(vt[:, m:m + 1], (tc, length)) for m in range(modes)], axis=0)


def conv_kernel(x_ref, g_ref, p_ref, o_ref):
    modes = p_ref.shape[1]
    tc, seg = x_ref.shape
    L = block_len
    shape = (modes, tc, L)
    rate = expand(p_ref[0], L)
    weight = expand(p_ref[1], L)
    state = expand(p_ref[2], L)
    rate_h = rate[:, :, :128]
    step_h = jnp.exp(-rate_h)
    end_h = jnp.exp(-rate_h * (L - 1.0))
    pos = lax.broadcasted_iota(jnp.int32, shape, 2).astype(jnp.float32)
    grow = jnp.exp(rate * pos)
    shrink = weight * jnp.exp(-rate * pos)
    step_decay = jnp.concatenate([step_h] * (L // 128), axis=2)
    block_decay = jnp.concatenate([end_h] * (L // 128), axis=2)
    first = pos == 0.0
    rows = lax.broadcasted_iota(jnp.int32, (L, L), 0)
    cols = lax.broadcasted_iota(jnp.int32, (L, L), 1)
    upper = (rows <= cols).astype(jnp.bfloat16)
    for b in range(seg // L):
        xb = x_ref[:, b * L:(b + 1) * L].astype(jnp.float32)
        u = xb[None] * grow + jnp.where(first, step_decay * state, 0.0)
        u2 = u.reshape(modes * tc, L)
        hi = u2.astype(jnp.bfloat16)
        lo = (u2 - hi.astype(jnp.float32)).astype(jnp.bfloat16)
        pre = jnp.dot(hi, upper, preferred_element_type=jnp.float32) + jnp.dot(
            lo, upper, preferred_element_type=jnp.float32
        )
        pre = pre.reshape(modes, tc, L)
        conv = jnp.sum(shrink * pre, axis=0)
        state = jnp.broadcast_to(pre[:, :, L - 1:L], shape) * block_decay
        gate = g_ref[:, b * L:(b + 1) * L].astype(jnp.float32)
        o_ref[:, b * L:(b + 1) * L] = (gate * conv).astype(o_ref.dtype)


def gated_conv(signal, gate, params):
    rows, seg = signal.shape
    modes = params.shape[1]
    tc = tile_ch
    return pl.pallas_call(
        conv_kernel,
        out_shape=jax.ShapeDtypeStruct((rows, seg), jnp.bfloat16),
        grid=(rows // tc,),
        in_specs=[
            pl.BlockSpec((tc, seg), lambda i: (i, 0)),
            pl.BlockSpec((tc, seg), lambda i: (i, 0)),
            pl.BlockSpec((3, modes, tc), lambda i: (0, 0, i)),
        ],
        out_specs=pl.BlockSpec((tc, seg), lambda i: (i, 0)),
        compiler_params=pltpu.CompilerParams(vmem_limit_bytes=48 * 1024 * 1024),
        cost_estimate=pl.CostEstimate(
            flops=4 * rows * seg * modes * block_len + 12 * rows * seg * modes,
            transcendentals=2 * rows * modes * block_len,
            bytes_accessed=6 * rows * seg + 3 * modes * rows * 4,
        ),
    )(signal, gate, params)


def end_kernel(x_ref, p_ref, o_ref):
    modes = p_ref.shape[1]
    tc, seg = x_ref.shape
    L = block_len
    nb = seg // L
    shape = (modes, tc, L)
    rate = expand(p_ref[0], L)
    pos = lax.broadcasted_iota(jnp.int32, shape, 2).astype(jnp.float32)
    tail = jnp.exp(-rate * (L - 1.0 - pos))
    whole = jnp.exp(-rate * float(L))
    total = jnp.zeros(shape, jnp.float32)
    for b in range(nb):
        xb = x_ref[:, b * L:(b + 1) * L].astype(jnp.float32)
        total = total * whole + xb[None] * tail
    ones = jnp.ones((8, L), jnp.bfloat16)
    dims = (((1,), (1,)), ((), ()))
    for m in range(modes):
        hi = total[m].astype(jnp.bfloat16)
        lo = (total[m] - hi.astype(jnp.float32)).astype(jnp.bfloat16)
        sums = lax.dot_general(ones, hi, dims, preferred_element_type=jnp.float32) + lax.dot_general(
            ones, lo, dims, preferred_element_type=jnp.float32
        )
        o_ref[m:m + 1, :] = sums[0:1, :]


def local_end_state(signal, params):
    rows, seg = signal.shape
    modes = params.shape[1]
    tc = tile_ch
    return pl.pallas_call(
        end_kernel,
        out_shape=jax.ShapeDtypeStruct((modes, rows), jnp.float32),
        grid=(rows // tc,),
        in_specs=[
            pl.BlockSpec((tc, seg), lambda i: (i, 0)),
            pl.BlockSpec((3, modes, tc), lambda i: (0, 0, i)),
        ],
        out_specs=pl.BlockSpec((modes, tc), lambda i: (0, i)),
        compiler_params=pltpu.CompilerParams(vmem_limit_bytes=48 * 1024 * 1024),
        cost_estimate=pl.CostEstimate(
            flops=3 * rows * seg * modes,
            transcendentals=2 * rows * block_len * modes,
            bytes_accessed=2 * rows * seg + 4 * modes * rows * 4,
        ),
    )(signal, params)


def per_device(residual_in, key_value, query_gate, decay_rates, residues, out_weight, norm_gain):
    rows, seg_len = key_value.shape
    n_seq = lax.axis_size("seq")
    total_len = n_seq * seg_len
    rates = decay_rates / total_len
    weights = residues * jnp.sqrt(2.0 * rates)
    zeros = jnp.zeros_like(rates.T)
    own_end = local_end_state(key_value, jnp.stack([rates.T, weights.T, zeros]))
    block_decay = jnp.exp(-rates.T * seg_len)

    def shifted(value, shift):
        return lax.ppermute(value, "seq", [(i, i + shift) for i in range(n_seq - shift)])

    carry_in = jnp.zeros_like(own_end)
    factor = jnp.ones_like(block_decay)
    for shift in range(1, 5):
        carry_in = carry_in + factor * shifted(own_end, shift)
        factor = factor * block_decay
    span = 4
    while span < n_seq:
        step = factor
        window = carry_in
        for q in range(1, 4):
            if q * span >= n_seq:
                break
            carry_in = carry_in + factor * shifted(window, q * span)
            factor = factor * step
        span *= 4
    packed = jnp.stack([rates.T, weights.T, carry_in])
    gated = gated_conv(key_value, query_gate, packed)
    summed = lax.psum_scatter(
        lax.dot_general(
            out_weight, gated, (((0,), (0,)), ((), ())), preferred_element_type=jnp.float32
        ).astype(jnp.bfloat16),
        "ch",
        scatter_dimension=0,
        tiled=True,
    ).astype(jnp.float32)
    mixed = residual_in.astype(jnp.float32) + summed
    squares = lax.psum(jnp.sum(mixed * mixed, axis=0), "ch")
    square_mean = squares / out_weight.shape[1]
    scaled = mixed * lax.rsqrt(square_mean + epsilon)[None, :] * norm_gain[:, None]
    return scaled.astype(jnp.bfloat16)


def solution(mesh):
    placed = (
        P("ch", "seq"),
        P("ch", "seq"),
        P("ch", "seq"),
        P("ch", None),
        P("ch", None),
        P("ch", None),
        P("ch"),
    )
    return jax.shard_map(
        per_device, mesh=mesh, in_specs=placed, out_specs=P("ch", "seq"), check_vma=False
    )
```

```python
import functools

import jax
import jax.numpy as jnp
from jax import lax
from jax.experimental import pallas as pl
from jax.experimental.pallas import tpu as pltpu
from jax.sharding import PartitionSpec as P

highest = lax.Precision.HIGHEST
epsilon = 1e-06
block_len = 256
tile_ch = 128


def expand(v, length):
    modes, tc = v.shape
    vt = v.T
    return jnp.stack([jnp.broadcast_to(vt[:, m:m + 1], (tc, length)) for m in range(modes)], axis=0)


def conv_kernel(x_ref, p_ref, o_ref):
    modes = p_ref.shape[1]
    tc, seg = x_ref.shape
    L = block_len
    shape = (modes, tc, L)
    rate = expand(p_ref[0], L)
    weight = expand(p_ref[1], L)
    rate_h = rate[:, :, :128]
    step_h = jnp.exp(-rate_h)
    end_h = jnp.exp(-rate_h * (L - 1.0))
    pos = lax.broadcasted_iota(jnp.int32, shape, 2).astype(jnp.float32)
    grow = jnp.exp(rate * pos)
    shrink = weight * jnp.exp(-rate * pos)
    step_decay = jnp.concatenate([step_h] * (L // 128), axis=2)
    block_decay = jnp.concatenate([end_h] * (L // 128), axis=2)
    first = pos == 0.0
    rows = lax.broadcasted_iota(jnp.int32, (L, L), 0)
    cols = lax.broadcasted_iota(jnp.int32, (L, L), 1)
    upper = (rows <= cols).astype(jnp.bfloat16)
    state = None
    for b in range(seg // L):
        xb = x_ref[:, b * L:(b + 1) * L].astype(jnp.float32)
        u = xb[None] * grow
        if state is not None:
            u = u + jnp.where(first, step_decay * state, 0.0)
        u2 = u.reshape(modes * tc, L)
        hi = u2.astype(jnp.bfloat16)
        lo = (u2 - hi.astype(jnp.float32)).astype(jnp.bfloat16)
        pre = jnp.dot(hi, upper, preferred_element_type=jnp.float32) + jnp.dot(
            lo, upper, preferred_element_type=jnp.float32
        )
        pre = pre.reshape(modes, tc, L)
        o_ref[:, b * L:(b + 1) * L] = jnp.sum(shrink * pre, axis=0)
        state = jnp.broadcast_to(pre[:, :, L - 1:L], shape) * block_decay


def local_conv(signal, params):
    rows, seg = signal.shape
    modes = params.shape[1]
    tc = tile_ch
    return pl.pallas_call(
        conv_kernel,
        out_shape=jax.ShapeDtypeStruct((rows, seg), jnp.float32),
        grid=(rows // tc,),
        in_specs=[
            pl.BlockSpec((tc, seg), lambda i: (i, 0)),
            pl.BlockSpec((3, modes, tc), lambda i: (0, 0, i)),
        ],
        out_specs=pl.BlockSpec((tc, seg), lambda i: (i, 0)),
        compiler_params=pltpu.CompilerParams(vmem_limit_bytes=48 * 1024 * 1024),
        cost_estimate=pl.CostEstimate(
            flops=4 * rows * seg * modes * block_len + 12 * rows * seg * modes,
            transcendentals=2 * rows * modes * block_len,
            bytes_accessed=6 * rows * seg + 3 * modes * rows * 4,
        ),
    )(signal, params)


def gate_kernel(c_ref, g_ref, p_ref, o_ref):
    modes = p_ref.shape[1]
    tc, seg = c_ref.shape
    L = block_len
    shape = (modes, tc, L)
    rate = expand(p_ref[0], L)
    coef = expand(p_ref[1], L) * expand(p_ref[2], L) * jnp.exp(-rate)
    pos = lax.broadcasted_iota(jnp.int32, shape, 2).astype(jnp.float32)
    decay = jnp.exp(-rate * pos)
    rate_h = rate[:, :, :128]
    whole_h = jnp.exp(-rate_h * float(L))
    whole = jnp.concatenate([whole_h] * (L // 128), axis=2)
    for b in range(seg // L):
        carry = jnp.sum(coef * decay, axis=0)
        conv = c_ref[:, b * L:(b + 1) * L] + carry
        gate = g_ref[:, b * L:(b + 1) * L].astype(jnp.float32)
        o_ref[:, b * L:(b + 1) * L] = (gate * conv).astype(o_ref.dtype)
        coef = coef * whole


def gated_conv(local, gate, params):
    rows, seg = local.shape
    modes = params.shape[1]
    tc = tile_ch
    return pl.pallas_call(
        gate_kernel,
        out_shape=jax.ShapeDtypeStruct((rows, seg), jnp.bfloat16),
        grid=(rows // tc,),
        in_specs=[
            pl.BlockSpec((tc, seg), lambda i: (i, 0)),
            pl.BlockSpec((tc, seg), lambda i: (i, 0)),
            pl.BlockSpec((3, modes, tc), lambda i: (0, 0, i)),
        ],
        out_specs=pl.BlockSpec((tc, seg), lambda i: (i, 0)),
        compiler_params=pltpu.CompilerParams(vmem_limit_bytes=48 * 1024 * 1024),
        cost_estimate=pl.CostEstimate(
            flops=3 * rows * seg * modes,
            transcendentals=rows * modes * block_len,
            bytes_accessed=8 * rows * seg + 3 * modes * rows * 4,
        ),
    )(local, gate, params)


def end_kernel(x_ref, p_ref, o_ref):
    modes = p_ref.shape[1]
    tc, seg = x_ref.shape
    L = block_len
    nb = seg // L
    shape = (modes, tc, L)
    rate = expand(p_ref[0], L)
    pos = lax.broadcasted_iota(jnp.int32, shape, 2).astype(jnp.float32)
    tail = jnp.exp(-rate * (L - 1.0 - pos))
    whole = jnp.exp(-rate * float(L))
    total = jnp.zeros(shape, jnp.float32)
    for b in range(nb):
        xb = x_ref[:, b * L:(b + 1) * L].astype(jnp.float32)
        total = total * whole + xb[None] * tail
    ones = jnp.ones((8, L), jnp.bfloat16)
    dims = (((1,), (1,)), ((), ()))
    for m in range(modes):
        hi = total[m].astype(jnp.bfloat16)
        lo = (total[m] - hi.astype(jnp.float32)).astype(jnp.bfloat16)
        sums = lax.dot_general(ones, hi, dims, preferred_element_type=jnp.float32) + lax.dot_general(
            ones, lo, dims, preferred_element_type=jnp.float32
        )
        o_ref[m:m + 1, :] = sums[0:1, :]


def local_end_state(signal, params):
    rows, seg = signal.shape
    modes = params.shape[1]
    tc = tile_ch
    return pl.pallas_call(
        end_kernel,
        out_shape=jax.ShapeDtypeStruct((modes, rows), jnp.float32),
        grid=(rows // tc,),
        in_specs=[
            pl.BlockSpec((tc, seg), lambda i: (i, 0)),
            pl.BlockSpec((3, modes, tc), lambda i: (0, 0, i)),
        ],
        out_specs=pl.BlockSpec((modes, tc), lambda i: (0, i)),
        compiler_params=pltpu.CompilerParams(vmem_limit_bytes=48 * 1024 * 1024),
        cost_estimate=pl.CostEstimate(
            flops=3 * rows * seg * modes,
            transcendentals=2 * rows * block_len * modes,
            bytes_accessed=2 * rows * seg + 4 * modes * rows * 4,
        ),
    )(signal, params)


def per_device(residual_in, key_value, query_gate, decay_rates, residues, out_weight, norm_gain):
    rows, seg_len = key_value.shape
    n_seq = lax.axis_size("seq")
    total_len = n_seq * seg_len
    rates = decay_rates / total_len
    weights = residues * jnp.sqrt(2.0 * rates)
    zeros = jnp.zeros_like(rates.T)
    own_end = local_end_state(key_value, jnp.stack([rates.T, weights.T, zeros]))
    local = local_conv(key_value, jnp.stack([rates.T, weights.T, zeros]))
    block_decay = jnp.exp(-rates.T * seg_len)

    def shifted(value, shift):
        return lax.ppermute(value, "seq", [(i, i + shift) for i in range(n_seq - shift)])

    carry_in = jnp.zeros_like(own_end)
    factor = jnp.ones_like(block_decay)
    for shift in range(1, 5):
        carry_in = carry_in + factor * shifted(own_end, shift)
        factor = factor * block_decay
    span = 4
    while span < n_seq:
        step = factor
        window = carry_in
        for q in range(1, 4):
            if q * span >= n_seq:
                break
            carry_in = carry_in + factor * shifted(window, q * span)
            factor = factor * step
        span *= 4
    packed = jnp.stack([rates.T, weights.T, carry_in])
    gated = gated_conv(local, query_gate, packed)
    summed = lax.psum_scatter(
        lax.dot_general(
            out_weight, gated, (((0,), (0,)), ((), ())), preferred_element_type=jnp.float32
        ).astype(jnp.bfloat16),
        "ch",
        scatter_dimension=0,
        tiled=True,
    ).astype(jnp.float32)
    mixed = residual_in.astype(jnp.float32) + summed
    squares = lax.psum(jnp.sum(mixed * mixed, axis=0), "ch")
    square_mean = squares / out_weight.shape[1]
    scaled = mixed * lax.rsqrt(square_mean + epsilon)[None, :] * norm_gain[:, None]
    return scaled.astype(jnp.bfloat16)


def solution(mesh):
    placed = (
        P("ch", "seq"),
        P("ch", "seq"),
        P("ch", "seq"),
        P("ch", None),
        P("ch", None),
        P("ch", None),
        P("ch"),
    )
    return jax.shard_map(
        per_device, mesh=mesh, in_specs=placed, out_specs=P("ch", "seq"), check_vma=False
    )
```

```python
import functools

import jax
import jax.numpy as jnp
from jax import lax
from jax.experimental import pallas as pl
from jax.experimental.pallas import tpu as pltpu
from jax.sharding import PartitionSpec as P

highest = lax.Precision.HIGHEST
epsilon = 1e-06
block_len = 256
tile_ch = 128


def expand(v, length):
    modes, tc = v.shape
    vt = v.T
    return jnp.stack([jnp.broadcast_to(vt[:, m:m + 1], (tc, length)) for m in range(modes)], axis=0)


def conv_kernel(x_ref, p_ref, o_ref):
    modes = p_ref.shape[1]
    tc, seg = x_ref.shape
    L = block_len
    shape = (modes, tc, L)
    rate = expand(p_ref[0], L)
    weight = expand(p_ref[1], L)
    rate_h = rate[:, :, :128]
    step_h = jnp.exp(-rate_h)
    end_h = jnp.exp(-rate_h * (L - 1.0))
    pos = lax.broadcasted_iota(jnp.int32, shape, 2).astype(jnp.float32)
    grow = jnp.exp(rate * pos)
    shrink = weight * jnp.exp(-rate * pos)
    step_decay = jnp.concatenate([step_h] * (L // 128), axis=2)
    block_decay = jnp.concatenate([end_h] * (L // 128), axis=2)
    first = pos == 0.0
    rows = lax.broadcasted_iota(jnp.int32, (L, L), 0)
    cols = lax.broadcasted_iota(jnp.int32, (L, L), 1)
    upper = (rows <= cols).astype(jnp.bfloat16)
    state = None
    for b in range(seg // L):
        xb = x_ref[:, b * L:(b + 1) * L].astype(jnp.float32)
        u = xb[None] * grow
        if state is not None:
            u = u + jnp.where(first, step_decay * state, 0.0)
        u2 = u.reshape(modes * tc, L)
        hi = u2.astype(jnp.bfloat16)
        lo = (u2 - hi.astype(jnp.float32)).astype(jnp.bfloat16)
        pre = jnp.dot(hi, upper, preferred_element_type=jnp.float32) + jnp.dot(
            lo, upper, preferred_element_type=jnp.float32
        )
        pre = pre.reshape(modes, tc, L)
        o_ref[:, b * L:(b + 1) * L] = jnp.sum(shrink * pre, axis=0)
        state = jnp.broadcast_to(pre[:, :, L - 1:L], shape) * block_decay


def local_conv(signal, params):
    rows, seg = signal.shape
    modes = params.shape[1]
    tc = tile_ch
    return pl.pallas_call(
        conv_kernel,
        out_shape=jax.ShapeDtypeStruct((rows, seg), jnp.float32),
        grid=(rows // tc,),
        in_specs=[
            pl.BlockSpec((tc, seg), lambda i: (i, 0)),
            pl.BlockSpec((3, modes, tc), lambda i: (0, 0, i)),
        ],
        out_specs=pl.BlockSpec((tc, seg), lambda i: (i, 0)),
        compiler_params=pltpu.CompilerParams(vmem_limit_bytes=48 * 1024 * 1024),
        cost_estimate=pl.CostEstimate(
            flops=4 * rows * seg * modes * block_len + 12 * rows * seg * modes,
            transcendentals=2 * rows * modes * block_len,
            bytes_accessed=6 * rows * seg + 3 * modes * rows * 4,
        ),
    )(signal, params)


def gate_kernel(c_ref, g_ref, p_ref, o_ref):
    modes = p_ref.shape[1]
    tc, seg = c_ref.shape
    L = block_len
    shape = (modes, tc, L)
    rate = expand(p_ref[0], L)
    coef = expand(p_ref[1], L) * expand(p_ref[2], L) * jnp.exp(-rate)
    pos = lax.broadcasted_iota(jnp.int32, shape, 2).astype(jnp.float32)
    decay = jnp.exp(-rate * pos)
    rate_h = rate[:, :, :128]
    whole_h = jnp.exp(-rate_h * float(L))
    whole = jnp.concatenate([whole_h] * (L // 128), axis=2)
    for b in range(seg // L):
        carry = jnp.sum(coef * decay, axis=0)
        conv = c_ref[:, b * L:(b + 1) * L] + carry
        gate = g_ref[:, b * L:(b + 1) * L].astype(jnp.float32)
        o_ref[:, b * L:(b + 1) * L] = (gate * conv).astype(o_ref.dtype)
        coef = coef * whole


def gated_conv(local, gate, params):
    rows, seg = local.shape
    modes = params.shape[1]
    tc = tile_ch
    return pl.pallas_call(
        gate_kernel,
        out_shape=jax.ShapeDtypeStruct((rows, seg), jnp.bfloat16),
        grid=(rows // tc,),
        in_specs=[
            pl.BlockSpec((tc, seg), lambda i: (i, 0)),
            pl.BlockSpec((tc, seg), lambda i: (i, 0)),
            pl.BlockSpec((3, modes, tc), lambda i: (0, 0, i)),
        ],
        out_specs=pl.BlockSpec((tc, seg), lambda i: (i, 0)),
        compiler_params=pltpu.CompilerParams(vmem_limit_bytes=48 * 1024 * 1024),
        cost_estimate=pl.CostEstimate(
            flops=3 * rows * seg * modes,
            transcendentals=rows * modes * block_len,
            bytes_accessed=8 * rows * seg + 3 * modes * rows * 4,
        ),
    )(local, gate, params)


def end_kernel(x_ref, p_ref, o_ref):
    modes = p_ref.shape[1]
    tc, seg = x_ref.shape
    L = block_len
    nb = seg // L
    shape = (modes, tc, L)
    rate = expand(p_ref[0], L)
    pos = lax.broadcasted_iota(jnp.int32, shape, 2).astype(jnp.float32)
    tail = jnp.exp(-rate * (L - 1.0 - pos))
    whole = jnp.exp(-rate * float(L))
    total = jnp.zeros(shape, jnp.float32)
    for b in range(nb):
        xb = x_ref[:, b * L:(b + 1) * L].astype(jnp.float32)
        total = total * whole + xb[None] * tail
    ones = jnp.ones((8, L), jnp.bfloat16)
    dims = (((1,), (1,)), ((), ()))
    for m in range(modes):
        hi = total[m].astype(jnp.bfloat16)
        lo = (total[m] - hi.astype(jnp.float32)).astype(jnp.bfloat16)
        sums = lax.dot_general(ones, hi, dims, preferred_element_type=jnp.float32) + lax.dot_general(
            ones, lo, dims, preferred_element_type=jnp.float32
        )
        o_ref[m:m + 1, :] = sums[0:1, :]


def local_end_state(signal, params):
    rows, seg = signal.shape
    modes = params.shape[1]
    tc = tile_ch
    return pl.pallas_call(
        end_kernel,
        out_shape=jax.ShapeDtypeStruct((modes, rows), jnp.float32),
        grid=(rows // tc,),
        in_specs=[
            pl.BlockSpec((tc, seg), lambda i: (i, 0)),
            pl.BlockSpec((3, modes, tc), lambda i: (0, 0, i)),
        ],
        out_specs=pl.BlockSpec((modes, tc), lambda i: (0, i)),
        compiler_params=pltpu.CompilerParams(vmem_limit_bytes=48 * 1024 * 1024),
        cost_estimate=pl.CostEstimate(
            flops=3 * rows * seg * modes,
            transcendentals=2 * rows * block_len * modes,
            bytes_accessed=2 * rows * seg + 4 * modes * rows * 4,
        ),
    )(signal, params)


def per_device(residual_in, key_value, query_gate, decay_rates, residues, out_weight, norm_gain):
    rows, seg_len = key_value.shape
    n_seq = lax.axis_size("seq")
    total_len = n_seq * seg_len
    rates = decay_rates / total_len
    weights = residues * jnp.sqrt(2.0 * rates)
    zeros = jnp.zeros_like(rates.T)
    own_end = local_end_state(key_value, jnp.stack([rates.T, weights.T, zeros]))
    local = local_conv(key_value, jnp.stack([rates.T, weights.T, zeros]))
    me = lax.axis_index("seq")
    later = jnp.arange(n_seq)
    gap = jnp.maximum(later - 1 - me, 0).astype(jnp.float32) * seg_len
    reach = jnp.where(
        (later > me)[:, None, None], jnp.exp(-rates.T[None] * gap[:, None, None]), 0.0
    )
    sent = reach * own_end[None]
    received = lax.all_to_all(sent, "seq", 0, 0, tiled=True)
    carry_in = jnp.sum(received, axis=0)
    packed = jnp.stack([rates.T, weights.T, carry_in])
    gated = gated_conv(local, query_gate, packed)
    summed = lax.psum_scatter(
        lax.dot_general(
            out_weight, gated, (((0,), (0,)), ((), ())), preferred_element_type=jnp.float32
        ).astype(jnp.bfloat16),
        "ch",
        scatter_dimension=0,
        tiled=True,
    ).astype(jnp.float32)
    mixed = residual_in.astype(jnp.float32) + summed
    squares = lax.psum(jnp.sum(mixed * mixed, axis=0), "ch")
    square_mean = squares / out_weight.shape[1]
    scaled = mixed * lax.rsqrt(square_mean + epsilon)[None, :] * norm_gain[:, None]
    return scaled.astype(jnp.bfloat16)


def solution(mesh):
    placed = (
        P("ch", "seq"),
        P("ch", "seq"),
        P("ch", "seq"),
        P("ch", None),
        P("ch", None),
        P("ch", None),
        P("ch"),
    )
    return jax.shard_map(
        per_device, mesh=mesh, in_specs=placed, out_specs=P("ch", "seq"), check_vma=False
    )
```

```python
import functools

import jax
import jax.numpy as jnp
from jax import lax
from jax.experimental import pallas as pl
from jax.experimental.pallas import tpu as pltpu
from jax.sharding import PartitionSpec as P

highest = lax.Precision.HIGHEST
epsilon = 1e-06
block_len = 256
tile_ch = 128


def expand(v, length):
    modes, tc = v.shape
    vt = v.T
    return jnp.stack([jnp.broadcast_to(vt[:, m:m + 1], (tc, length)) for m in range(modes)], axis=0)


def conv_kernel(x_ref, p_ref, o_ref):
    modes = p_ref.shape[1]
    tc, seg = x_ref.shape
    L = block_len
    shape = (modes, tc, L)
    rate = expand(p_ref[0], L)
    weight = expand(p_ref[1], L)
    rate_h = rate[:, :, :128]
    step_h = jnp.exp(-rate_h)
    end_h = jnp.exp(-rate_h * (L - 1.0))
    pos = lax.broadcasted_iota(jnp.int32, shape, 2).astype(jnp.float32)
    grow = jnp.exp(rate * pos)
    shrink = weight * jnp.exp(-rate * pos)
    step_decay = jnp.concatenate([step_h] * (L // 128), axis=2)
    block_decay = jnp.concatenate([end_h] * (L // 128), axis=2)
    first = pos == 0.0
    rows = lax.broadcasted_iota(jnp.int32, (L, L), 0)
    cols = lax.broadcasted_iota(jnp.int32, (L, L), 1)
    upper = (rows <= cols).astype(jnp.bfloat16)
    state = None
    for b in range(seg // L):
        xb = x_ref[:, b * L:(b + 1) * L].astype(jnp.float32)
        u = xb[None] * grow
        if state is not None:
            u = u + jnp.where(first, step_decay * state, 0.0)
        u2 = u.reshape(modes * tc, L)
        hi = u2.astype(jnp.bfloat16)
        lo = (u2 - hi.astype(jnp.float32)).astype(jnp.bfloat16)
        pre = jnp.dot(hi, upper, preferred_element_type=jnp.float32) + jnp.dot(
            lo, upper, preferred_element_type=jnp.float32
        )
        pre = pre.reshape(modes, tc, L)
        o_ref[:, b * L:(b + 1) * L] = jnp.sum(shrink * pre, axis=0)
        state = jnp.broadcast_to(pre[:, :, L - 1:L], shape) * block_decay


def local_conv(signal, params):
    rows, seg = signal.shape
    modes = params.shape[1]
    tc = tile_ch
    return pl.pallas_call(
        conv_kernel,
        out_shape=jax.ShapeDtypeStruct((rows, seg), jnp.float32),
        grid=(rows // tc,),
        in_specs=[
            pl.BlockSpec((tc, seg), lambda i: (i, 0)),
            pl.BlockSpec((3, modes, tc), lambda i: (0, 0, i)),
        ],
        out_specs=pl.BlockSpec((tc, seg), lambda i: (i, 0)),
        compiler_params=pltpu.CompilerParams(vmem_limit_bytes=48 * 1024 * 1024),
        cost_estimate=pl.CostEstimate(
            flops=4 * rows * seg * modes * block_len + 12 * rows * seg * modes,
            transcendentals=2 * rows * modes * block_len,
            bytes_accessed=6 * rows * seg + 3 * modes * rows * 4,
        ),
    )(signal, params)


def gate_kernel(c_ref, g_ref, p_ref, o_ref):
    modes = p_ref.shape[1]
    tc, seg = c_ref.shape
    L = block_len
    shape = (modes, tc, L)
    rate = expand(p_ref[0], L)
    coef = expand(p_ref[1], L) * expand(p_ref[2], L) * jnp.exp(-rate)
    pos = lax.broadcasted_iota(jnp.int32, shape, 2).astype(jnp.float32)
    decay = jnp.exp(-rate * pos)
    rate_h = rate[:, :, :128]
    whole_h = jnp.exp(-rate_h * float(L))
    whole = jnp.concatenate([whole_h] * (L // 128), axis=2)
    for b in range(seg // L):
        carry = jnp.sum(coef * decay, axis=0)
        conv = c_ref[:, b * L:(b + 1) * L] + carry
        gate = g_ref[:, b * L:(b + 1) * L].astype(jnp.float32)
        o_ref[:, b * L:(b + 1) * L] = (gate * conv).astype(o_ref.dtype)
        coef = coef * whole


def gated_conv(local, gate, params):
    rows, seg = local.shape
    modes = params.shape[1]
    tc = tile_ch
    return pl.pallas_call(
        gate_kernel,
        out_shape=jax.ShapeDtypeStruct((rows, seg), jnp.bfloat16),
        grid=(rows // tc,),
        in_specs=[
            pl.BlockSpec((tc, seg), lambda i: (i, 0)),
            pl.BlockSpec((tc, seg), lambda i: (i, 0)),
            pl.BlockSpec((3, modes, tc), lambda i: (0, 0, i)),
        ],
        out_specs=pl.BlockSpec((tc, seg), lambda i: (i, 0)),
        compiler_params=pltpu.CompilerParams(vmem_limit_bytes=48 * 1024 * 1024),
        cost_estimate=pl.CostEstimate(
            flops=3 * rows * seg * modes,
            transcendentals=rows * modes * block_len,
            bytes_accessed=8 * rows * seg + 3 * modes * rows * 4,
        ),
    )(local, gate, params)


def end_kernel(x_ref, p_ref, o_ref):
    modes = p_ref.shape[1]
    tc, seg = x_ref.shape
    L = block_len
    nb = seg // L
    shape = (modes, tc, L)
    rate = expand(p_ref[0], L)
    pos = lax.broadcasted_iota(jnp.int32, shape, 2).astype(jnp.float32)
    tail = jnp.exp(-rate * (L - 1.0 - pos))
    whole = jnp.exp(-rate * float(L))
    total = jnp.zeros(shape, jnp.float32)
    for b in range(nb):
        xb = x_ref[:, b * L:(b + 1) * L].astype(jnp.float32)
        total = total * whole + xb[None] * tail
    ones = jnp.ones((8, L), jnp.bfloat16)
    dims = (((1,), (1,)), ((), ()))
    for m in range(modes):
        hi = total[m].astype(jnp.bfloat16)
        lo = (total[m] - hi.astype(jnp.float32)).astype(jnp.bfloat16)
        sums = lax.dot_general(ones, hi, dims, preferred_element_type=jnp.float32) + lax.dot_general(
            ones, lo, dims, preferred_element_type=jnp.float32
        )
        o_ref[m:m + 1, :] = sums[0:1, :]


def local_end_state(signal, params):
    rows, seg = signal.shape
    modes = params.shape[1]
    tc = tile_ch
    return pl.pallas_call(
        end_kernel,
        out_shape=jax.ShapeDtypeStruct((modes, rows), jnp.float32),
        grid=(rows // tc,),
        in_specs=[
            pl.BlockSpec((tc, seg), lambda i: (i, 0)),
            pl.BlockSpec((3, modes, tc), lambda i: (0, 0, i)),
        ],
        out_specs=pl.BlockSpec((modes, tc), lambda i: (0, i)),
        compiler_params=pltpu.CompilerParams(vmem_limit_bytes=48 * 1024 * 1024),
        cost_estimate=pl.CostEstimate(
            flops=3 * rows * seg * modes,
            transcendentals=2 * rows * block_len * modes,
            bytes_accessed=2 * rows * seg + 4 * modes * rows * 4,
        ),
    )(signal, params)


def per_device(residual_in, key_value, query_gate, decay_rates, residues, out_weight, norm_gain):
    rows, seg_len = key_value.shape
    n_seq = lax.axis_size("seq")
    total_len = n_seq * seg_len
    rates = decay_rates / total_len
    weights = residues * jnp.sqrt(2.0 * rates)
    zeros = jnp.zeros_like(rates.T)
    own_end = local_end_state(key_value, jnp.stack([rates.T, weights.T, zeros]))
    local = local_conv(key_value, jnp.stack([rates.T, weights.T, zeros]))
    me = lax.axis_index("seq")
    later = jnp.arange(n_seq)
    gap = jnp.maximum(later - 1 - me, 0).astype(jnp.float32) * seg_len
    reach = jnp.where(
        (later > me)[:, None, None], jnp.exp(-rates.T[None] * gap[:, None, None]), 0.0
    )
    sent = reach * own_end[None]
    received = lax.all_to_all(sent, "seq", 0, 0, tiled=True)
    carry_in = jnp.sum(received, axis=0)
    packed = jnp.stack([rates.T, weights.T, carry_in])
    gated = gated_conv(local, query_gate, packed)
    summed = lax.psum_scatter(
        lax.dot_general(
            out_weight, gated, (((0,), (0,)), ((), ())), preferred_element_type=jnp.float32
        ).astype(jnp.bfloat16),
        "ch",
        scatter_dimension=0,
        tiled=True,
    ).astype(jnp.float32)
    mixed = residual_in.astype(jnp.float32) + summed
    squares = jnp.sum(mixed * mixed, axis=0)
    n_ch = lax.axis_size("ch")
    partner = 1
    while partner < n_ch:
        squares = squares + lax.ppermute(squares, "ch", [(k, k ^ partner) for k in range(n_ch)])
        partner *= 2
    square_mean = squares / out_weight.shape[1]
    scaled = mixed * lax.rsqrt(square_mean + epsilon)[None, :] * norm_gain[:, None]
    return scaled.astype(jnp.bfloat16)


def solution(mesh):
    placed = (
        P("ch", "seq"),
        P("ch", "seq"),
        P("ch", "seq"),
        P("ch", None),
        P("ch", None),
        P("ch", None),
        P("ch"),
    )
    return jax.shard_map(
        per_device, mesh=mesh, in_specs=placed, out_specs=P("ch", "seq"), check_vma=False
    )
```

```python
import functools

import jax
import jax.numpy as jnp
from jax import lax
from jax.experimental import pallas as pl
from jax.experimental.pallas import tpu as pltpu
from jax.sharding import PartitionSpec as P

highest = lax.Precision.HIGHEST
epsilon = 1e-06
block_len = 256
tile_ch = 128


def expand(v, length):
    modes, tc = v.shape
    vt = v.T
    return jnp.stack([jnp.broadcast_to(vt[:, m:m + 1], (tc, length)) for m in range(modes)], axis=0)


def conv_kernel(x_ref, p_ref, o_ref):
    modes = p_ref.shape[1]
    tc, seg = x_ref.shape
    L = block_len
    shape = (modes, tc, L)
    rate = expand(p_ref[0], L)
    weight = expand(p_ref[1], L)
    rate_h = rate[:, :, :128]
    step_h = jnp.exp(-rate_h)
    end_h = jnp.exp(-rate_h * (L - 1.0))
    pos = lax.broadcasted_iota(jnp.int32, shape, 2).astype(jnp.float32)
    grow = jnp.exp(rate * pos)
    shrink = weight * jnp.exp(-rate * pos)
    step_decay = jnp.concatenate([step_h] * (L // 128), axis=2)
    block_decay = jnp.concatenate([end_h] * (L // 128), axis=2)
    first = pos == 0.0
    rows = lax.broadcasted_iota(jnp.int32, (L, L), 0)
    cols = lax.broadcasted_iota(jnp.int32, (L, L), 1)
    upper = (rows <= cols).astype(jnp.bfloat16)
    state = None
    for b in range(seg // L):
        xb = x_ref[:, b * L:(b + 1) * L].astype(jnp.float32)
        u = xb[None] * grow
        if state is not None:
            u = u + jnp.where(first, step_decay * state, 0.0)
        u2 = u.reshape(modes * tc, L)
        hi = u2.astype(jnp.bfloat16)
        lo = (u2 - hi.astype(jnp.float32)).astype(jnp.bfloat16)
        pre = jnp.dot(hi, upper, preferred_element_type=jnp.float32) + jnp.dot(
            lo, upper, preferred_element_type=jnp.float32
        )
        pre = pre.reshape(modes, tc, L)
        o_ref[:, b * L:(b + 1) * L] = jnp.sum(shrink * pre, axis=0)
        state = jnp.broadcast_to(pre[:, :, L - 1:L], shape) * block_decay


def local_conv(signal, params):
    rows, seg = signal.shape
    modes = params.shape[1]
    tc = tile_ch
    return pl.pallas_call(
        conv_kernel,
        out_shape=jax.ShapeDtypeStruct((rows, seg), jnp.float32),
        grid=(rows // tc,),
        in_specs=[
            pl.BlockSpec((tc, seg), lambda i: (i, 0)),
            pl.BlockSpec((3, modes, tc), lambda i: (0, 0, i)),
        ],
        out_specs=pl.BlockSpec((tc, seg), lambda i: (i, 0)),
        compiler_params=pltpu.CompilerParams(vmem_limit_bytes=48 * 1024 * 1024),
        cost_estimate=pl.CostEstimate(
            flops=4 * rows * seg * modes * block_len + 12 * rows * seg * modes,
            transcendentals=2 * rows * modes * block_len,
            bytes_accessed=6 * rows * seg + 3 * modes * rows * 4,
        ),
    )(signal, params)


def gate_kernel(c_ref, g_ref, p_ref, o_ref):
    modes = p_ref.shape[1]
    tc, seg = c_ref.shape
    L = block_len
    shape = (modes, tc, L)
    rate_h = expand(p_ref[0], 128)
    pos_h = lax.broadcasted_iota(jnp.int32, (modes, tc, 128), 2).astype(jnp.float32)
    decay_h = jnp.exp(-rate_h * pos_h)
    half_h = jnp.exp(-rate_h * 128.0)
    coef_h = expand(p_ref[1], 128) * expand(p_ref[2], 128) * jnp.exp(-rate_h)
    decay = jnp.concatenate([decay_h, decay_h * half_h], axis=2)
    coef = jnp.concatenate([coef_h, coef_h], axis=2)
    whole_h = half_h * half_h
    whole = jnp.concatenate([whole_h, whole_h], axis=2)
    for b in range(seg // L):
        carry = jnp.sum(coef * decay, axis=0)
        conv = c_ref[:, b * L:(b + 1) * L] + carry
        gate = g_ref[:, b * L:(b + 1) * L].astype(jnp.float32)
        o_ref[:, b * L:(b + 1) * L] = (gate * conv).astype(o_ref.dtype)
        coef = coef * whole


def gated_conv(local, gate, params):
    rows, seg = local.shape
    modes = params.shape[1]
    tc = tile_ch
    return pl.pallas_call(
        gate_kernel,
        out_shape=jax.ShapeDtypeStruct((rows, seg), jnp.bfloat16),
        grid=(rows // tc,),
        in_specs=[
            pl.BlockSpec((tc, seg), lambda i: (i, 0)),
            pl.BlockSpec((tc, seg), lambda i: (i, 0)),
            pl.BlockSpec((3, modes, tc), lambda i: (0, 0, i)),
        ],
        out_specs=pl.BlockSpec((tc, seg), lambda i: (i, 0)),
        compiler_params=pltpu.CompilerParams(vmem_limit_bytes=48 * 1024 * 1024),
        cost_estimate=pl.CostEstimate(
            flops=3 * rows * seg * modes,
            transcendentals=rows * modes * block_len,
            bytes_accessed=8 * rows * seg + 3 * modes * rows * 4,
        ),
    )(local, gate, params)


def end_kernel(x_ref, p_ref, o_ref):
    modes = p_ref.shape[1]
    tc, seg = x_ref.shape
    L = block_len
    nb = seg // L
    shape = (modes, tc, L)
    rate_h = expand(p_ref[0], 128)
    pos_h = lax.broadcasted_iota(jnp.int32, (modes, tc, 128), 2).astype(jnp.float32)
    tail_h = jnp.exp(-rate_h * (127.0 - pos_h))
    half_h = jnp.exp(-rate_h * 128.0)
    tail = jnp.concatenate([tail_h * half_h, tail_h], axis=2)
    whole_h = half_h * half_h
    whole = jnp.concatenate([whole_h, whole_h], axis=2)
    total = jnp.zeros(shape, jnp.float32)
    for b in range(nb):
        xb = x_ref[:, b * L:(b + 1) * L].astype(jnp.float32)
        total = total * whole + xb[None] * tail
    ones = jnp.ones((8, L), jnp.bfloat16)
    dims = (((1,), (1,)), ((), ()))
    for m in range(modes):
        hi = total[m].astype(jnp.bfloat16)
        lo = (total[m] - hi.astype(jnp.float32)).astype(jnp.bfloat16)
        sums = lax.dot_general(ones, hi, dims, preferred_element_type=jnp.float32) + lax.dot_general(
            ones, lo, dims, preferred_element_type=jnp.float32
        )
        o_ref[m:m + 1, :] = sums[0:1, :]


def local_end_state(signal, params):
    rows, seg = signal.shape
    modes = params.shape[1]
    tc = tile_ch
    return pl.pallas_call(
        end_kernel,
        out_shape=jax.ShapeDtypeStruct((modes, rows), jnp.float32),
        grid=(rows // tc,),
        in_specs=[
            pl.BlockSpec((tc, seg), lambda i: (i, 0)),
            pl.BlockSpec((3, modes, tc), lambda i: (0, 0, i)),
        ],
        out_specs=pl.BlockSpec((modes, tc), lambda i: (0, i)),
        compiler_params=pltpu.CompilerParams(vmem_limit_bytes=48 * 1024 * 1024),
        cost_estimate=pl.CostEstimate(
            flops=3 * rows * seg * modes,
            transcendentals=2 * rows * block_len * modes,
            bytes_accessed=2 * rows * seg + 4 * modes * rows * 4,
        ),
    )(signal, params)


def per_device(residual_in, key_value, query_gate, decay_rates, residues, out_weight, norm_gain):
    rows, seg_len = key_value.shape
    n_seq = lax.axis_size("seq")
    total_len = n_seq * seg_len
    rates = decay_rates / total_len
    weights = residues * jnp.sqrt(2.0 * rates)
    zeros = jnp.zeros_like(rates.T)
    own_end = local_end_state(key_value, jnp.stack([rates.T, weights.T, zeros]))
    local = local_conv(key_value, jnp.stack([rates.T, weights.T, zeros]))
    me = lax.axis_index("seq")
    later = jnp.arange(n_seq)
    gap = jnp.maximum(later - 1 - me, 0).astype(jnp.float32) * seg_len
    reach = jnp.where(
        (later > me)[:, None, None], jnp.exp(-rates.T[None] * gap[:, None, None]), 0.0
    )
    sent = reach * own_end[None]
    received = lax.all_to_all(sent, "seq", 0, 0, tiled=True)
    carry_in = jnp.sum(received, axis=0)
    packed = jnp.stack([rates.T, weights.T, carry_in])
    gated = gated_conv(local, query_gate, packed)
    summed = lax.psum_scatter(
        lax.dot_general(
            out_weight, gated, (((0,), (0,)), ((), ())), preferred_element_type=jnp.float32
        ).astype(jnp.bfloat16),
        "ch",
        scatter_dimension=0,
        tiled=True,
    ).astype(jnp.float32)
    mixed = residual_in.astype(jnp.float32) + summed
    squares = jnp.sum(mixed * mixed, axis=0)
    n_ch = lax.axis_size("ch")
    partner = 1
    while partner < n_ch:
        squares = squares + lax.ppermute(squares, "ch", [(k, k ^ partner) for k in range(n_ch)])
        partner *= 2
    square_mean = squares / out_weight.shape[1]
    scaled = mixed * lax.rsqrt(square_mean + epsilon)[None, :] * norm_gain[:, None]
    return scaled.astype(jnp.bfloat16)


def solution(mesh):
    placed = (
        P("ch", "seq"),
        P("ch", "seq"),
        P("ch", "seq"),
        P("ch", None),
        P("ch", None),
        P("ch", None),
        P("ch"),
    )
    return jax.shard_map(
        per_device, mesh=mesh, in_specs=placed, out_specs=P("ch", "seq"), check_vma=False
    )
```

```python
import functools

import jax
import jax.numpy as jnp
from jax import lax
from jax.experimental import pallas as pl
from jax.experimental.pallas import tpu as pltpu
from jax.sharding import PartitionSpec as P

highest = lax.Precision.HIGHEST
epsilon = 1e-06
block_len = 256
tile_ch = 128


def expand(v, length):
    modes, tc = v.shape
    vt = v.T
    return jnp.stack([jnp.broadcast_to(vt[:, m:m + 1], (tc, length)) for m in range(modes)], axis=0)


def conv_kernel(x_ref, p_ref, o_ref):
    modes = p_ref.shape[1]
    tc, seg = x_ref.shape
    L = block_len
    shape = (modes, tc, L)
    rate = expand(p_ref[0], L)
    weight = expand(p_ref[1], L)
    rate_h = rate[:, :, :128]
    step_h = jnp.exp(-rate_h)
    end_h = jnp.exp(-rate_h * (L - 1.0))
    pos = lax.broadcasted_iota(jnp.int32, shape, 2).astype(jnp.float32)
    grow = jnp.exp(rate * pos)
    shrink = weight * jnp.exp(-rate * pos)
    step_decay = jnp.concatenate([step_h] * (L // 128), axis=2)
    block_decay = jnp.concatenate([end_h] * (L // 128), axis=2)
    first = pos == 0.0
    rows = lax.broadcasted_iota(jnp.int32, (L, L), 0)
    cols = lax.broadcasted_iota(jnp.int32, (L, L), 1)
    upper = (rows <= cols).astype(jnp.bfloat16)
    state = None
    for b in range(seg // L):
        xb = x_ref[:, b * L:(b + 1) * L].astype(jnp.float32)
        u = xb[None] * grow
        if state is not None:
            u = u + jnp.where(first, step_decay * state, 0.0)
        u2 = u.reshape(modes * tc, L)
        hi = u2.astype(jnp.bfloat16)
        lo = (u2 - hi.astype(jnp.float32)).astype(jnp.bfloat16)
        pre = jnp.dot(hi, upper, preferred_element_type=jnp.float32) + jnp.dot(
            lo, upper, preferred_element_type=jnp.float32
        )
        pre = pre.reshape(modes, tc, L)
        o_ref[:, b * L:(b + 1) * L] = jnp.sum(shrink * pre, axis=0)
        state = jnp.broadcast_to(pre[:, :, L - 1:L], shape) * block_decay


def local_conv(signal, params):
    rows, seg = signal.shape
    modes = params.shape[1]
    tc = tile_ch
    return pl.pallas_call(
        conv_kernel,
        out_shape=jax.ShapeDtypeStruct((rows, seg), jnp.float32),
        grid=(rows // tc,),
        in_specs=[
            pl.BlockSpec((tc, seg), lambda i: (i, 0)),
            pl.BlockSpec((3, modes, tc), lambda i: (0, 0, i)),
        ],
        out_specs=pl.BlockSpec((tc, seg), lambda i: (i, 0)),
        compiler_params=pltpu.CompilerParams(vmem_limit_bytes=48 * 1024 * 1024),
        cost_estimate=pl.CostEstimate(
            flops=4 * rows * seg * modes * block_len + 12 * rows * seg * modes,
            transcendentals=2 * rows * modes * block_len,
            bytes_accessed=6 * rows * seg + 3 * modes * rows * 4,
        ),
    )(signal, params)


def gate_kernel(c_ref, g_ref, p_ref, o_ref):
    modes = p_ref.shape[1]
    tc, seg = c_ref.shape
    L = block_len
    shape = (modes, tc, L)
    rate_h = expand(p_ref[0], 128)
    pos_h = lax.broadcasted_iota(jnp.int32, (modes, tc, 128), 2).astype(jnp.float32)
    decay_h = jnp.exp(-rate_h * pos_h)
    half_h = jnp.exp(-rate_h * 128.0)
    coef_h = expand(p_ref[1], 128) * expand(p_ref[2], 128) * jnp.exp(-rate_h)
    decay = jnp.concatenate([decay_h, decay_h * half_h], axis=2)
    coef = jnp.concatenate([coef_h, coef_h], axis=2)
    whole_h = half_h * half_h
    whole = jnp.concatenate([whole_h, whole_h], axis=2)
    for b in range(seg // L):
        carry = jnp.sum(coef * decay, axis=0)
        conv = c_ref[:, b * L:(b + 1) * L] + carry
        gate = g_ref[:, b * L:(b + 1) * L].astype(jnp.float32)
        o_ref[:, b * L:(b + 1) * L] = (gate * conv).astype(o_ref.dtype)
        coef = coef * whole


def gate_project_kernel(c_ref, g_ref, p_ref, w_ref, o_ref, gated_ref, acc_ref):
    i = pl.program_id(0)
    gate_kernel(c_ref, g_ref, p_ref, gated_ref)
    part = jnp.dot(w_ref[...], gated_ref[...], preferred_element_type=jnp.float32)

    @pl.when(i == 0)
    def _():
        acc_ref[...] = part

    @pl.when(i > 0)
    def _():
        acc_ref[...] += part

    @pl.when(i == pl.num_programs(0) - 1)
    def _():
        o_ref[...] = acc_ref[...].astype(o_ref.dtype)


def gated_project(local, gate, params, weight_t):
    rows, seg = local.shape
    modes = params.shape[1]
    outs = weight_t.shape[0]
    tc = tile_ch
    return pl.pallas_call(
        gate_project_kernel,
        out_shape=jax.ShapeDtypeStruct((outs, seg), jnp.bfloat16),
        grid=(rows // tc,),
        in_specs=[
            pl.BlockSpec((tc, seg), lambda i: (i, 0)),
            pl.BlockSpec((tc, seg), lambda i: (i, 0)),
            pl.BlockSpec((3, modes, tc), lambda i: (0, 0, i)),
            pl.BlockSpec((outs, tc), lambda i: (0, i)),
        ],
        out_specs=pl.BlockSpec((outs, seg), lambda i: (0, 0)),
        scratch_shapes=[
            pltpu.VMEM((tc, seg), jnp.bfloat16),
            pltpu.VMEM((outs, seg), jnp.float32),
        ],
        compiler_params=pltpu.CompilerParams(
            vmem_limit_bytes=62 * 1024 * 1024, dimension_semantics=("arbitrary",)
        ),
        cost_estimate=pl.CostEstimate(
            flops=2 * rows * seg * outs + 3 * rows * seg * modes,
            transcendentals=rows * modes * block_len,
            bytes_accessed=7 * rows * seg + 2 * rows * outs + 2 * outs * seg,
        ),
    )(local, gate, params, weight_t)


def end_kernel(x_ref, p_ref, o_ref):
    modes = p_ref.shape[1]
    tc, seg = x_ref.shape
    L = block_len
    nb = seg // L
    shape = (modes, tc, L)
    rate_h = expand(p_ref[0], 128)
    pos_h = lax.broadcasted_iota(jnp.int32, (modes, tc, 128), 2).astype(jnp.float32)
    tail_h = jnp.exp(-rate_h * (127.0 - pos_h))
    half_h = jnp.exp(-rate_h * 128.0)
    tail = jnp.concatenate([tail_h * half_h, tail_h], axis=2)
    whole_h = half_h * half_h
    whole = jnp.concatenate([whole_h, whole_h], axis=2)
    total = jnp.zeros(shape, jnp.float32)
    for b in range(nb):
        xb = x_ref[:, b * L:(b + 1) * L].astype(jnp.float32)
        total = total * whole + xb[None] * tail
    ones = jnp.ones((8, L), jnp.bfloat16)
    dims = (((1,), (1,)), ((), ()))
    for m in range(modes):
        hi = total[m].astype(jnp.bfloat16)
        lo = (total[m] - hi.astype(jnp.float32)).astype(jnp.bfloat16)
        sums = lax.dot_general(ones, hi, dims, preferred_element_type=jnp.float32) + lax.dot_general(
            ones, lo, dims, preferred_element_type=jnp.float32
        )
        o_ref[m:m + 1, :] = sums[0:1, :]


def local_end_state(signal, params):
    rows, seg = signal.shape
    modes = params.shape[1]
    tc = tile_ch
    return pl.pallas_call(
        end_kernel,
        out_shape=jax.ShapeDtypeStruct((modes, rows), jnp.float32),
        grid=(rows // tc,),
        in_specs=[
            pl.BlockSpec((tc, seg), lambda i: (i, 0)),
            pl.BlockSpec((3, modes, tc), lambda i: (0, 0, i)),
        ],
        out_specs=pl.BlockSpec((modes, tc), lambda i: (0, i)),
        compiler_params=pltpu.CompilerParams(vmem_limit_bytes=48 * 1024 * 1024),
        cost_estimate=pl.CostEstimate(
            flops=3 * rows * seg * modes,
            transcendentals=2 * rows * block_len * modes,
            bytes_accessed=2 * rows * seg + 4 * modes * rows * 4,
        ),
    )(signal, params)


def per_device(residual_in, key_value, query_gate, decay_rates, residues, out_weight, norm_gain):
    rows, seg_len = key_value.shape
    n_seq = lax.axis_size("seq")
    total_len = n_seq * seg_len
    rates = decay_rates / total_len
    weights = residues * jnp.sqrt(2.0 * rates)
    zeros = jnp.zeros_like(rates.T)
    own_end = local_end_state(key_value, jnp.stack([rates.T, weights.T, zeros]))
    local = local_conv(key_value, jnp.stack([rates.T, weights.T, zeros]))
    me = lax.axis_index("seq")
    later = jnp.arange(n_seq)
    gap = jnp.maximum(later - 1 - me, 0).astype(jnp.float32) * seg_len
    reach = jnp.where(
        (later > me)[:, None, None], jnp.exp(-rates.T[None] * gap[:, None, None]), 0.0
    )
    sent = reach * own_end[None]
    received = lax.all_to_all(sent, "seq", 0, 0, tiled=True)
    carry_in = jnp.sum(received, axis=0)
    packed = jnp.stack([rates.T, weights.T, carry_in])
    part = gated_project(local, query_gate, packed, out_weight.T)
    summed = lax.psum_scatter(part, "ch", scatter_dimension=0, tiled=True).astype(jnp.float32)
    mixed = residual_in.astype(jnp.float32) + summed
    squares = jnp.sum(mixed * mixed, axis=0)
    n_ch = lax.axis_size("ch")
    partner = 1
    while partner < n_ch:
        squares = squares + lax.ppermute(squares, "ch", [(k, k ^ partner) for k in range(n_ch)])
        partner *= 2
    square_mean = squares / out_weight.shape[1]
    scaled = mixed * lax.rsqrt(square_mean + epsilon)[None, :] * norm_gain[:, None]
    return scaled.astype(jnp.bfloat16)


def solution(mesh):
    placed = (
        P("ch", "seq"),
        P("ch", "seq"),
        P("ch", "seq"),
        P("ch", None),
        P("ch", None),
        P("ch", None),
        P("ch"),
    )
    return jax.shard_map(
        per_device, mesh=mesh, in_specs=placed, out_specs=P("ch", "seq"), check_vma=False
    )
```

```python
import functools

import jax
import jax.numpy as jnp
from jax import lax
from jax.experimental import pallas as pl
from jax.experimental.pallas import tpu as pltpu
from jax.sharding import PartitionSpec as P

highest = lax.Precision.HIGHEST
epsilon = 1e-06
block_len = 256
tile_ch = 128


def expand(v, length):
    modes, tc = v.shape
    vt = v.T
    return jnp.stack([jnp.broadcast_to(vt[:, m:m + 1], (tc, length)) for m in range(modes)], axis=0)


def conv_kernel(x_ref, p_ref, o_ref):
    modes = p_ref.shape[1]
    tc, seg = x_ref.shape
    L = block_len
    shape = (modes, tc, L)
    rate = expand(p_ref[0], L)
    weight = expand(p_ref[1], L)
    rate_h = rate[:, :, :128]
    step_h = jnp.exp(-rate_h)
    end_h = jnp.exp(-rate_h * (L - 1.0))
    pos = lax.broadcasted_iota(jnp.int32, shape, 2).astype(jnp.float32)
    grow = jnp.exp(rate * pos)
    shrink = weight * jnp.exp(-rate * pos)
    step_decay = jnp.concatenate([step_h] * (L // 128), axis=2)
    block_decay = jnp.concatenate([end_h] * (L // 128), axis=2)
    first = pos == 0.0
    rows = lax.broadcasted_iota(jnp.int32, (L, L), 0)
    cols = lax.broadcasted_iota(jnp.int32, (L, L), 1)
    upper = (rows <= cols).astype(jnp.bfloat16)
    state = None
    for b in range(seg // L):
        xb = x_ref[:, b * L:(b + 1) * L].astype(jnp.float32)
        u = xb[None] * grow
        if state is not None:
            u = u + jnp.where(first, step_decay * state, 0.0)
        u2 = u.reshape(modes * tc, L)
        hi = u2.astype(jnp.bfloat16)
        lo = (u2 - hi.astype(jnp.float32)).astype(jnp.bfloat16)
        pre = jnp.dot(hi, upper, preferred_element_type=jnp.float32) + jnp.dot(
            lo, upper, preferred_element_type=jnp.float32
        )
        pre = pre.reshape(modes, tc, L)
        o_ref[:, b * L:(b + 1) * L] = jnp.sum(shrink * pre, axis=0)
        state = jnp.broadcast_to(pre[:, :, L - 1:L], shape) * block_decay


def local_conv(signal, params):
    rows, seg = signal.shape
    modes = params.shape[1]
    tc = tile_ch
    return pl.pallas_call(
        conv_kernel,
        out_shape=jax.ShapeDtypeStruct((rows, seg), jnp.float32),
        grid=(rows // tc,),
        in_specs=[
            pl.BlockSpec((tc, seg), lambda i: (i, 0)),
            pl.BlockSpec((3, modes, tc), lambda i: (0, 0, i)),
        ],
        out_specs=pl.BlockSpec((tc, seg), lambda i: (i, 0)),
        compiler_params=pltpu.CompilerParams(vmem_limit_bytes=48 * 1024 * 1024),
        cost_estimate=pl.CostEstimate(
            flops=4 * rows * seg * modes * block_len + 12 * rows * seg * modes,
            transcendentals=2 * rows * modes * block_len,
            bytes_accessed=6 * rows * seg + 3 * modes * rows * 4,
        ),
    )(signal, params)


def gate_kernel(c_ref, g_ref, p_ref, r_ref, o_ref):
    modes = p_ref.shape[1]
    tc, seg = c_ref.shape
    L = block_len
    shape = (modes, tc, L)
    rate_h = expand(p_ref[0], 128)
    pos_h = lax.broadcasted_iota(jnp.int32, (modes, tc, 128), 2).astype(jnp.float32)
    decay_h = jnp.exp(-rate_h * pos_h)
    half_h = jnp.exp(-rate_h * 128.0)
    carry_in = jnp.sum(r_ref[...], axis=0)
    coef_h = expand(p_ref[1], 128) * expand(carry_in, 128) * jnp.exp(-rate_h)
    decay = jnp.concatenate([decay_h, decay_h * half_h], axis=2)
    coef = jnp.concatenate([coef_h, coef_h], axis=2)
    whole_h = half_h * half_h
    whole = jnp.concatenate([whole_h, whole_h], axis=2)
    for b in range(seg // L):
        carry = jnp.sum(coef * decay, axis=0)
        conv = c_ref[:, b * L:(b + 1) * L] + carry
        gate = g_ref[:, b * L:(b + 1) * L].astype(jnp.float32)
        o_ref[:, b * L:(b + 1) * L] = (gate * conv).astype(o_ref.dtype)
        coef = coef * whole


def gated_conv(local, gate, params, received):
    rows, seg = local.shape
    modes = params.shape[1]
    n_src = received.shape[0]
    tc = tile_ch
    return pl.pallas_call(
        gate_kernel,
        out_shape=jax.ShapeDtypeStruct((rows, seg), jnp.bfloat16),
        grid=(rows // tc,),
        in_specs=[
            pl.BlockSpec((tc, seg), lambda i: (i, 0)),
            pl.BlockSpec((tc, seg), lambda i: (i, 0)),
            pl.BlockSpec((2, modes, tc), lambda i: (0, 0, i)),
            pl.BlockSpec((n_src, modes, tc), lambda i: (0, 0, i)),
        ],
        out_specs=pl.BlockSpec((tc, seg), lambda i: (i, 0)),
        compiler_params=pltpu.CompilerParams(vmem_limit_bytes=48 * 1024 * 1024),
        cost_estimate=pl.CostEstimate(
            flops=3 * rows * seg * modes,
            transcendentals=rows * modes * block_len,
            bytes_accessed=8 * rows * seg + (2 + n_src) * modes * rows * 4,
        ),
    )(local, gate, params, received)


def end_kernel(x_ref, p_ref, o_ref):
    modes = p_ref.shape[1]
    tc, seg = x_ref.shape
    L = block_len
    nb = seg // L
    shape = (modes, tc, L)
    rate_h = expand(p_ref[0], 128)
    pos_h = lax.broadcasted_iota(jnp.int32, (modes, tc, 128), 2).astype(jnp.float32)
    tail_h = jnp.exp(-rate_h * (127.0 - pos_h))
    half_h = jnp.exp(-rate_h * 128.0)
    tail = jnp.concatenate([tail_h * half_h, tail_h], axis=2)
    whole_h = half_h * half_h
    whole = jnp.concatenate([whole_h, whole_h], axis=2)
    total = jnp.zeros(shape, jnp.float32)
    for b in range(nb):
        xb = x_ref[:, b * L:(b + 1) * L].astype(jnp.float32)
        total = total * whole + xb[None] * tail
    ones = jnp.ones((8, L), jnp.bfloat16)
    dims = (((1,), (1,)), ((), ()))
    for m in range(modes):
        hi = total[m].astype(jnp.bfloat16)
        lo = (total[m] - hi.astype(jnp.float32)).astype(jnp.bfloat16)
        sums = lax.dot_general(ones, hi, dims, preferred_element_type=jnp.float32) + lax.dot_general(
            ones, lo, dims, preferred_element_type=jnp.float32
        )
        o_ref[m:m + 1, :] = sums[0:1, :]


def local_end_state(signal, params):
    rows, seg = signal.shape
    modes = params.shape[1]
    tc = tile_ch
    return pl.pallas_call(
        end_kernel,
        out_shape=jax.ShapeDtypeStruct((modes, rows), jnp.float32),
        grid=(rows // tc,),
        in_specs=[
            pl.BlockSpec((tc, seg), lambda i: (i, 0)),
            pl.BlockSpec((3, modes, tc), lambda i: (0, 0, i)),
        ],
        out_specs=pl.BlockSpec((modes, tc), lambda i: (0, i)),
        compiler_params=pltpu.CompilerParams(vmem_limit_bytes=48 * 1024 * 1024),
        cost_estimate=pl.CostEstimate(
            flops=3 * rows * seg * modes,
            transcendentals=2 * rows * block_len * modes,
            bytes_accessed=2 * rows * seg + 4 * modes * rows * 4,
        ),
    )(signal, params)


def per_device(residual_in, key_value, query_gate, decay_rates, residues, out_weight, norm_gain):
    rows, seg_len = key_value.shape
    n_seq = lax.axis_size("seq")
    total_len = n_seq * seg_len
    rates = decay_rates / total_len
    weights = residues * jnp.sqrt(2.0 * rates)
    zeros = jnp.zeros_like(rates.T)
    own_end = local_end_state(key_value, jnp.stack([rates.T, weights.T, zeros]))
    local = local_conv(key_value, jnp.stack([rates.T, weights.T, zeros]))
    me = lax.axis_index("seq")
    later = jnp.arange(n_seq)
    gap = jnp.maximum(later - 1 - me, 0).astype(jnp.float32) * seg_len
    reach = jnp.where(
        (later > me)[:, None, None], jnp.exp(-rates.T[None] * gap[:, None, None]), 0.0
    )
    sent = reach * own_end[None]
    received = lax.all_to_all(sent, "seq", 0, 0, tiled=True)
    gated = gated_conv(local, query_gate, jnp.stack([rates.T, weights.T]), received)
    summed = lax.psum_scatter(
        lax.dot_general(
            out_weight, gated, (((0,), (0,)), ((), ())), preferred_element_type=jnp.float32
        ).astype(jnp.bfloat16),
        "ch",
        scatter_dimension=0,
        tiled=True,
    ).astype(jnp.float32)
    mixed = residual_in.astype(jnp.float32) + summed
    squares = jnp.sum(mixed * mixed, axis=0)
    n_ch = lax.axis_size("ch")
    partner = 1
    while partner < n_ch:
        squares = squares + lax.ppermute(squares, "ch", [(k, k ^ partner) for k in range(n_ch)])
        partner *= 2
    square_mean = squares / out_weight.shape[1]
    scaled = mixed * lax.rsqrt(square_mean + epsilon)[None, :] * norm_gain[:, None]
    return scaled.astype(jnp.bfloat16)


def solution(mesh):
    placed = (
        P("ch", "seq"),
        P("ch", "seq"),
        P("ch", "seq"),
        P("ch", None),
        P("ch", None),
        P("ch", None),
        P("ch"),
    )
    return jax.shard_map(
        per_device, mesh=mesh, in_specs=placed, out_specs=P("ch", "seq"), check_vma=False
    )
```

```python
import functools

import jax
import jax.numpy as jnp
from jax import lax
from jax.experimental import pallas as pl
from jax.experimental.pallas import tpu as pltpu
from jax.sharding import PartitionSpec as P

highest = lax.Precision.HIGHEST
epsilon = 1e-06
block_len = 256
tile_ch = 128


def expand(v, length):
    modes, tc = v.shape
    vt = v.T
    return jnp.stack([jnp.broadcast_to(vt[:, m:m + 1], (tc, length)) for m in range(modes)], axis=0)


def conv_kernel(x_ref, p_ref, o_ref):
    modes = p_ref.shape[1]
    tc, seg = x_ref.shape
    L = block_len
    shape = (modes, tc, L)
    rate = expand(p_ref[0], L)
    weight = expand(p_ref[1], L)
    rate_h = rate[:, :, :128]
    step_h = jnp.exp(-rate_h)
    end_h = jnp.exp(-rate_h * (L - 1.0))
    pos = lax.broadcasted_iota(jnp.int32, shape, 2).astype(jnp.float32)
    grow = jnp.exp(rate * pos)
    shrink = weight * jnp.exp(-rate * pos)
    step_decay = jnp.concatenate([step_h] * (L // 128), axis=2)
    block_decay = jnp.concatenate([end_h] * (L // 128), axis=2)
    first = pos == 0.0
    rows = lax.broadcasted_iota(jnp.int32, (L, L), 0)
    cols = lax.broadcasted_iota(jnp.int32, (L, L), 1)
    upper = (rows <= cols).astype(jnp.bfloat16)
    state = None
    for b in range(seg // L):
        xb = x_ref[:, b * L:(b + 1) * L].astype(jnp.float32)
        u = xb[None] * grow
        if state is not None:
            u = u + jnp.where(first, step_decay * state, 0.0)
        u2 = u.reshape(modes * tc, L)
        hi = u2.astype(jnp.bfloat16)
        lo = (u2 - hi.astype(jnp.float32)).astype(jnp.bfloat16)
        pre = jnp.dot(hi, upper, preferred_element_type=jnp.float32) + jnp.dot(
            lo, upper, preferred_element_type=jnp.float32
        )
        pre = pre.reshape(modes, tc, L)
        o_ref[:, b * L:(b + 1) * L] = jnp.sum(shrink * pre, axis=0)
        state = jnp.broadcast_to(pre[:, :, L - 1:L], shape) * block_decay


def local_conv(signal, params):
    rows, seg = signal.shape
    modes = params.shape[1]
    tc = tile_ch
    return pl.pallas_call(
        conv_kernel,
        out_shape=jax.ShapeDtypeStruct((rows, seg), jnp.float32),
        grid=(rows // tc,),
        in_specs=[
            pl.BlockSpec((tc, seg), lambda i: (i, 0)),
            pl.BlockSpec((3, modes, tc), lambda i: (0, 0, i)),
        ],
        out_specs=pl.BlockSpec((tc, seg), lambda i: (i, 0)),
        compiler_params=pltpu.CompilerParams(vmem_limit_bytes=48 * 1024 * 1024),
        cost_estimate=pl.CostEstimate(
            flops=4 * rows * seg * modes * block_len + 12 * rows * seg * modes,
            transcendentals=2 * rows * modes * block_len,
            bytes_accessed=6 * rows * seg + 3 * modes * rows * 4,
        ),
    )(signal, params)


def gate_kernel(c_ref, g_ref, p_ref, o_ref):
    modes = p_ref.shape[1]
    tc, seg = c_ref.shape
    L = block_len
    shape = (modes, tc, L)
    rate_h = expand(p_ref[0], 128)
    pos_h = lax.broadcasted_iota(jnp.int32, (modes, tc, 128), 2).astype(jnp.float32)
    decay_h = jnp.exp(-rate_h * pos_h)
    half_h = jnp.exp(-rate_h * 128.0)
    coef_h = expand(p_ref[1], 128) * expand(p_ref[2], 128) * jnp.exp(-rate_h)
    decay = jnp.concatenate([decay_h, decay_h * half_h], axis=2)
    coef = jnp.concatenate([coef_h, coef_h], axis=2)
    whole_h = half_h * half_h
    whole = jnp.concatenate([whole_h, whole_h], axis=2)
    for b in range(seg // L):
        carry = jnp.sum(coef * decay, axis=0)
        conv = c_ref[:, b * L:(b + 1) * L] + carry
        gate = g_ref[:, b * L:(b + 1) * L].astype(jnp.float32)
        o_ref[:, b * L:(b + 1) * L] = (gate * conv).astype(o_ref.dtype)
        coef = coef * whole


def gated_conv(local, gate, params):
    rows, seg = local.shape
    modes = params.shape[1]
    tc = tile_ch
    return pl.pallas_call(
        gate_kernel,
        out_shape=jax.ShapeDtypeStruct((rows, seg), jnp.bfloat16),
        grid=(rows // tc,),
        in_specs=[
            pl.BlockSpec((tc, seg), lambda i: (i, 0)),
            pl.BlockSpec((tc, seg), lambda i: (i, 0)),
            pl.BlockSpec((3, modes, tc), lambda i: (0, 0, i)),
        ],
        out_specs=pl.BlockSpec((tc, seg), lambda i: (i, 0)),
        compiler_params=pltpu.CompilerParams(vmem_limit_bytes=48 * 1024 * 1024),
        cost_estimate=pl.CostEstimate(
            flops=3 * rows * seg * modes,
            transcendentals=rows * modes * block_len,
            bytes_accessed=8 * rows * seg + 3 * modes * rows * 4,
        ),
    )(local, gate, params)


def end_kernel(x_ref, p_ref, o_ref):
    modes = p_ref.shape[1]
    tc, seg = x_ref.shape
    L = block_len
    nb = seg // L
    shape = (modes, tc, L)
    rate_h = expand(p_ref[0], 128)
    pos_h = lax.broadcasted_iota(jnp.int32, (modes, tc, 128), 2).astype(jnp.float32)
    tail_h = jnp.exp(-rate_h * (127.0 - pos_h))
    half_h = jnp.exp(-rate_h * 128.0)
    tail = jnp.concatenate([tail_h * half_h, tail_h], axis=2)
    whole_h = half_h * half_h
    whole = jnp.concatenate([whole_h, whole_h], axis=2)
    total = jnp.zeros(shape, jnp.float32)
    for b in range(nb):
        xb = x_ref[:, b * L:(b + 1) * L].astype(jnp.float32)
        total = total * whole + xb[None] * tail
    o_ref[...] = jnp.sum(total, axis=2)


def local_end_state(signal, params):
    rows, seg = signal.shape
    modes = params.shape[1]
    tc = tile_ch
    return pl.pallas_call(
        end_kernel,
        out_shape=jax.ShapeDtypeStruct((modes, rows), jnp.float32),
        grid=(rows // tc,),
        in_specs=[
            pl.BlockSpec((tc, seg), lambda i: (i, 0)),
            pl.BlockSpec((3, modes, tc), lambda i: (0, 0, i)),
        ],
        out_specs=pl.BlockSpec((modes, tc), lambda i: (0, i)),
        compiler_params=pltpu.CompilerParams(vmem_limit_bytes=48 * 1024 * 1024),
        cost_estimate=pl.CostEstimate(
            flops=3 * rows * seg * modes,
            transcendentals=2 * rows * block_len * modes,
            bytes_accessed=2 * rows * seg + 4 * modes * rows * 4,
        ),
    )(signal, params)


def per_device(residual_in, key_value, query_gate, decay_rates, residues, out_weight, norm_gain):
    rows, seg_len = key_value.shape
    n_seq = lax.axis_size("seq")
    total_len = n_seq * seg_len
    rates = decay_rates / total_len
    weights = residues * jnp.sqrt(2.0 * rates)
    zeros = jnp.zeros_like(rates.T)
    own_end = local_end_state(key_value, jnp.stack([rates.T, weights.T, zeros]))
    local = local_conv(key_value, jnp.stack([rates.T, weights.T, zeros]))
    me = lax.axis_index("seq")
    later = jnp.arange(n_seq)
    gap = jnp.maximum(later - 1 - me, 0).astype(jnp.float32) * seg_len
    reach = jnp.where(
        (later > me)[:, None, None], jnp.exp(-rates.T[None] * gap[:, None, None]), 0.0
    )
    sent = reach * own_end[None]
    received = lax.all_to_all(sent, "seq", 0, 0, tiled=True)
    carry_in = jnp.sum(received, axis=0)
    packed = jnp.stack([rates.T, weights.T, carry_in])
    gated = gated_conv(local, query_gate, packed)
    summed = lax.psum_scatter(
        lax.dot_general(
            out_weight, gated, (((0,), (0,)), ((), ())), preferred_element_type=jnp.float32
        ).astype(jnp.bfloat16),
        "ch",
        scatter_dimension=0,
        tiled=True,
    ).astype(jnp.float32)
    mixed = residual_in.astype(jnp.float32) + summed
    squares = jnp.sum(mixed * mixed, axis=0)
    n_ch = lax.axis_size("ch")
    partner = 1
    while partner < n_ch:
        squares = squares + lax.ppermute(squares, "ch", [(k, k ^ partner) for k in range(n_ch)])
        partner *= 2
    square_mean = squares / out_weight.shape[1]
    scaled = mixed * lax.rsqrt(square_mean + epsilon)[None, :] * norm_gain[:, None]
    return scaled.astype(jnp.bfloat16)


def solution(mesh):
    placed = (
        P("ch", "seq"),
        P("ch", "seq"),
        P("ch", "seq"),
        P("ch", None),
        P("ch", None),
        P("ch", None),
        P("ch"),
    )
    return jax.shard_map(
        per_device, mesh=mesh, in_specs=placed, out_specs=P("ch", "seq"), check_vma=False
    )
```

```python
import functools

import jax
import jax.numpy as jnp
from jax import lax
from jax.experimental import pallas as pl
from jax.experimental.pallas import tpu as pltpu
from jax.sharding import PartitionSpec as P

highest = lax.Precision.HIGHEST
epsilon = 1e-06
block_len = 256
tile_ch = 128


def expand(v, length):
    modes, tc = v.shape
    vt = v.T
    return jnp.stack([jnp.broadcast_to(vt[:, m:m + 1], (tc, length)) for m in range(modes)], axis=0)


def conv_kernel(x_ref, p_ref, o_ref):
    modes = p_ref.shape[1]
    tc, seg = x_ref.shape
    L = block_len
    shape = (modes, tc, L)
    rate = expand(p_ref[0], L)
    weight = expand(p_ref[1], L)
    rate_h = rate[:, :, :128]
    step_h = jnp.exp(-rate_h)
    end_h = jnp.exp(-rate_h * (L - 1.0))
    pos = lax.broadcasted_iota(jnp.int32, shape, 2).astype(jnp.float32)
    grow = jnp.exp(rate * pos)
    shrink = weight * jnp.exp(-rate * pos)
    step_decay = jnp.concatenate([step_h] * (L // 128), axis=2)
    block_decay = jnp.concatenate([end_h] * (L // 128), axis=2)
    first = pos == 0.0
    rows = lax.broadcasted_iota(jnp.int32, (L, L), 0)
    cols = lax.broadcasted_iota(jnp.int32, (L, L), 1)
    upper = (rows <= cols).astype(jnp.bfloat16)
    state = None
    for b in range(seg // L):
        xb = x_ref[:, b * L:(b + 1) * L].astype(jnp.float32)
        u = xb[None] * grow
        if state is not None:
            u = u + jnp.where(first, step_decay * state, 0.0)
        u2 = u.reshape(modes * tc, L)
        hi = u2.astype(jnp.bfloat16)
        lo = (u2 - hi.astype(jnp.float32)).astype(jnp.bfloat16)
        pre = jnp.dot(hi, upper, preferred_element_type=jnp.float32) + jnp.dot(
            lo, upper, preferred_element_type=jnp.float32
        )
        pre = pre.reshape(modes, tc, L)
        o_ref[:, b * L:(b + 1) * L] = jnp.sum(shrink * pre, axis=0)
        state = jnp.broadcast_to(pre[:, :, L - 1:L], shape) * block_decay


def local_conv(signal, params):
    rows, seg = signal.shape
    modes = params.shape[1]
    tc = tile_ch
    return pl.pallas_call(
        conv_kernel,
        out_shape=jax.ShapeDtypeStruct((rows, seg), jnp.float32),
        grid=(rows // tc,),
        in_specs=[
            pl.BlockSpec((tc, seg), lambda i: (i, 0)),
            pl.BlockSpec((3, modes, tc), lambda i: (0, 0, i)),
        ],
        out_specs=pl.BlockSpec((tc, seg), lambda i: (i, 0)),
        compiler_params=pltpu.CompilerParams(vmem_limit_bytes=48 * 1024 * 1024),
        cost_estimate=pl.CostEstimate(
            flops=4 * rows * seg * modes * block_len + 12 * rows * seg * modes,
            transcendentals=2 * rows * modes * block_len,
            bytes_accessed=6 * rows * seg + 3 * modes * rows * 4,
        ),
    )(signal, params)


def gate_kernel(c_ref, g_ref, p_ref, o_ref):
    modes = p_ref.shape[1]
    tc, seg = c_ref.shape
    L = block_len
    shape = (modes, tc, L)
    rate_h = expand(p_ref[0], 128)
    pos_h = lax.broadcasted_iota(jnp.int32, (modes, tc, 128), 2).astype(jnp.float32)
    decay_h = jnp.exp(-rate_h * pos_h)
    half_h = jnp.exp(-rate_h * 128.0)
    coef_h = expand(p_ref[1], 128) * expand(p_ref[2], 128) * jnp.exp(-rate_h)
    decay = jnp.concatenate([decay_h, decay_h * half_h], axis=2)
    coef = jnp.concatenate([coef_h, coef_h], axis=2)
    whole_h = half_h * half_h
    whole = jnp.concatenate([whole_h, whole_h], axis=2)
    for b in range(seg // L):
        carry = jnp.sum(coef * decay, axis=0)
        conv = c_ref[:, b * L:(b + 1) * L] + carry
        gate = g_ref[:, b * L:(b + 1) * L].astype(jnp.float32)
        o_ref[:, b * L:(b + 1) * L] = (gate * conv).astype(o_ref.dtype)
        coef = coef * whole


def gated_conv(local, gate, params):
    rows, seg = local.shape
    modes = params.shape[1]
    tc = tile_ch
    return pl.pallas_call(
        gate_kernel,
        out_shape=jax.ShapeDtypeStruct((rows, seg), jnp.bfloat16),
        grid=(rows // tc,),
        in_specs=[
            pl.BlockSpec((tc, seg), lambda i: (i, 0)),
            pl.BlockSpec((tc, seg), lambda i: (i, 0)),
            pl.BlockSpec((3, modes, tc), lambda i: (0, 0, i)),
        ],
        out_specs=pl.BlockSpec((tc, seg), lambda i: (i, 0)),
        compiler_params=pltpu.CompilerParams(vmem_limit_bytes=48 * 1024 * 1024),
        cost_estimate=pl.CostEstimate(
            flops=3 * rows * seg * modes,
            transcendentals=rows * modes * block_len,
            bytes_accessed=8 * rows * seg + 3 * modes * rows * 4,
        ),
    )(local, gate, params)


def end_kernel(x_ref, p_ref, o_ref):
    modes = p_ref.shape[1]
    tc, seg = x_ref.shape
    L = block_len
    nb = seg // L
    shape = (modes, tc, L)
    rate_h = expand(p_ref[0], 128)
    pos_h = lax.broadcasted_iota(jnp.int32, (modes, tc, 128), 2).astype(jnp.float32)
    tail_h = jnp.exp(-rate_h * (127.0 - pos_h))
    half_h = jnp.exp(-rate_h * 128.0)
    tail = jnp.concatenate([tail_h * half_h, tail_h], axis=2)
    whole_h = half_h * half_h
    whole = jnp.concatenate([whole_h, whole_h], axis=2)
    total = jnp.zeros(shape, jnp.float32)
    for b in range(nb):
        xb = x_ref[:, b * L:(b + 1) * L].astype(jnp.float32)
        total = total * whole + xb[None] * tail
    o_ref[...] = jnp.sum(total, axis=2)


def local_end_state(signal, params):
    rows, seg = signal.shape
    modes = params.shape[1]
    tc = 2 * tile_ch
    return pl.pallas_call(
        end_kernel,
        out_shape=jax.ShapeDtypeStruct((modes, rows), jnp.float32),
        grid=(rows // tc,),
        in_specs=[
            pl.BlockSpec((tc, seg), lambda i: (i, 0)),
            pl.BlockSpec((3, modes, tc), lambda i: (0, 0, i)),
        ],
        out_specs=pl.BlockSpec((modes, tc), lambda i: (0, i)),
        compiler_params=pltpu.CompilerParams(vmem_limit_bytes=48 * 1024 * 1024),
        cost_estimate=pl.CostEstimate(
            flops=3 * rows * seg * modes,
            transcendentals=2 * rows * block_len * modes,
            bytes_accessed=2 * rows * seg + 4 * modes * rows * 4,
        ),
    )(signal, params)


def per_device(residual_in, key_value, query_gate, decay_rates, residues, out_weight, norm_gain):
    rows, seg_len = key_value.shape
    n_seq = lax.axis_size("seq")
    total_len = n_seq * seg_len
    rates = decay_rates / total_len
    weights = residues * jnp.sqrt(2.0 * rates)
    zeros = jnp.zeros_like(rates.T)
    own_end = local_end_state(key_value, jnp.stack([rates.T, weights.T, zeros]))
    local = local_conv(key_value, jnp.stack([rates.T, weights.T, zeros]))
    me = lax.axis_index("seq")
    later = jnp.arange(n_seq)
    gap = jnp.maximum(later - 1 - me, 0).astype(jnp.float32) * seg_len
    reach = jnp.where(
        (later > me)[:, None, None], jnp.exp(-rates.T[None] * gap[:, None, None]), 0.0
    )
    sent = reach * own_end[None]
    received = lax.all_to_all(sent, "seq", 0, 0, tiled=True)
    carry_in = jnp.sum(received, axis=0)
    packed = jnp.stack([rates.T, weights.T, carry_in])
    gated = gated_conv(local, query_gate, packed)
    summed = lax.psum_scatter(
        lax.dot_general(
            out_weight, gated, (((0,), (0,)), ((), ())), preferred_element_type=jnp.float32
        ).astype(jnp.bfloat16),
        "ch",
        scatter_dimension=0,
        tiled=True,
    ).astype(jnp.float32)
    mixed = residual_in.astype(jnp.float32) + summed
    squares = jnp.sum(mixed * mixed, axis=0)
    n_ch = lax.axis_size("ch")
    partner = 1
    while partner < n_ch:
        squares = squares + lax.ppermute(squares, "ch", [(k, k ^ partner) for k in range(n_ch)])
        partner *= 2
    square_mean = squares / out_weight.shape[1]
    scaled = mixed * lax.rsqrt(square_mean + epsilon)[None, :] * norm_gain[:, None]
    return scaled.astype(jnp.bfloat16)


def solution(mesh):
    placed = (
        P("ch", "seq"),
        P("ch", "seq"),
        P("ch", "seq"),
        P("ch", None),
        P("ch", None),
        P("ch", None),
        P("ch"),
    )
    return jax.shard_map(
        per_device, mesh=mesh, in_specs=placed, out_specs=P("ch", "seq"), check_vma=False
    )
```

```python
import functools

import jax
import jax.numpy as jnp
from jax import lax
from jax.experimental import pallas as pl
from jax.experimental.pallas import tpu as pltpu
from jax.sharding import PartitionSpec as P

highest = lax.Precision.HIGHEST
epsilon = 1e-06
block_len = 256
tile_ch = 128


def expand(v, length):
    modes, tc = v.shape
    vt = v.T
    return jnp.stack([jnp.broadcast_to(vt[:, m:m + 1], (tc, length)) for m in range(modes)], axis=0)


def conv_kernel(x_ref, p_ref, o_ref):
    modes = p_ref.shape[1]
    tc, seg = x_ref.shape
    L = block_len
    shape = (modes, tc, L)
    rate = expand(p_ref[0], L)
    weight = expand(p_ref[1], L)
    rate_h = rate[:, :, :128]
    step_h = jnp.exp(-rate_h)
    end_h = jnp.exp(-rate_h * (L - 1.0))
    pos = lax.broadcasted_iota(jnp.int32, shape, 2).astype(jnp.float32)
    grow = jnp.exp(rate * pos)
    shrink = weight * jnp.exp(-rate * pos)
    step_decay = jnp.concatenate([step_h] * (L // 128), axis=2)
    block_decay = jnp.concatenate([end_h] * (L // 128), axis=2)
    first = pos == 0.0
    rows = lax.broadcasted_iota(jnp.int32, (L, L), 0)
    cols = lax.broadcasted_iota(jnp.int32, (L, L), 1)
    upper = (rows <= cols).astype(jnp.bfloat16)
    state = None
    for b in range(seg // L):
        xb = x_ref[:, b * L:(b + 1) * L].astype(jnp.float32)
        u = xb[None] * grow
        if state is not None:
            u = u + jnp.where(first, step_decay * state, 0.0)
        u2 = u.reshape(modes * tc, L)
        hi = u2.astype(jnp.bfloat16)
        lo = (u2 - hi.astype(jnp.float32)).astype(jnp.bfloat16)
        pre = jnp.dot(hi, upper, preferred_element_type=jnp.float32) + jnp.dot(
            lo, upper, preferred_element_type=jnp.float32
        )
        pre = pre.reshape(modes, tc, L)
        o_ref[:, b * L:(b + 1) * L] = jnp.sum(shrink * pre, axis=0)
        state = jnp.broadcast_to(pre[:, :, L - 1:L], shape) * block_decay


def local_conv(signal, params):
    rows, seg = signal.shape
    modes = params.shape[1]
    tc = tile_ch
    return pl.pallas_call(
        conv_kernel,
        out_shape=jax.ShapeDtypeStruct((rows, seg), jnp.float32),
        grid=(rows // tc,),
        in_specs=[
            pl.BlockSpec((tc, seg), lambda i: (i, 0)),
            pl.BlockSpec((3, modes, tc), lambda i: (0, 0, i)),
        ],
        out_specs=pl.BlockSpec((tc, seg), lambda i: (i, 0)),
        compiler_params=pltpu.CompilerParams(vmem_limit_bytes=48 * 1024 * 1024),
        cost_estimate=pl.CostEstimate(
            flops=4 * rows * seg * modes * block_len + 12 * rows * seg * modes,
            transcendentals=2 * rows * modes * block_len,
            bytes_accessed=6 * rows * seg + 3 * modes * rows * 4,
        ),
    )(signal, params)


def gate_kernel(c_ref, g_ref, p_ref, o_ref):
    modes = p_ref.shape[1]
    tc, seg = c_ref.shape
    L = block_len
    shape = (modes, tc, L)
    rate_h = expand(p_ref[0], 128)
    pos_h = lax.broadcasted_iota(jnp.int32, (modes, tc, 128), 2).astype(jnp.float32)
    decay_h = jnp.exp(-rate_h * pos_h)
    half_h = jnp.exp(-rate_h * 128.0)
    coef_h = expand(p_ref[1], 128) * expand(p_ref[2], 128) * jnp.exp(-rate_h)
    decay = jnp.concatenate([decay_h, decay_h * half_h], axis=2)
    coef = jnp.concatenate([coef_h, coef_h], axis=2)
    whole_h = half_h * half_h
    whole = jnp.concatenate([whole_h, whole_h], axis=2)
    for b in range(seg // L):
        carry = jnp.sum(coef * decay, axis=0)
        conv = c_ref[:, b * L:(b + 1) * L] + carry
        gate = g_ref[:, b * L:(b + 1) * L].astype(jnp.float32)
        o_ref[:, b * L:(b + 1) * L] = (gate * conv).astype(o_ref.dtype)
        coef = coef * whole


def gated_conv(local, gate, params):
    rows, seg = local.shape
    modes = params.shape[1]
    tc = 2 * tile_ch
    return pl.pallas_call(
        gate_kernel,
        out_shape=jax.ShapeDtypeStruct((rows, seg), jnp.bfloat16),
        grid=(rows // tc,),
        in_specs=[
            pl.BlockSpec((tc, seg), lambda i: (i, 0)),
            pl.BlockSpec((tc, seg), lambda i: (i, 0)),
            pl.BlockSpec((3, modes, tc), lambda i: (0, 0, i)),
        ],
        out_specs=pl.BlockSpec((tc, seg), lambda i: (i, 0)),
        compiler_params=pltpu.CompilerParams(vmem_limit_bytes=48 * 1024 * 1024),
        cost_estimate=pl.CostEstimate(
            flops=3 * rows * seg * modes,
            transcendentals=rows * modes * block_len,
            bytes_accessed=8 * rows * seg + 3 * modes * rows * 4,
        ),
    )(local, gate, params)


def end_kernel(x_ref, p_ref, o_ref):
    modes = p_ref.shape[1]
    tc, seg = x_ref.shape
    L = block_len
    nb = seg // L
    shape = (modes, tc, L)
    rate_h = expand(p_ref[0], 128)
    pos_h = lax.broadcasted_iota(jnp.int32, (modes, tc, 128), 2).astype(jnp.float32)
    tail_h = jnp.exp(-rate_h * (127.0 - pos_h))
    half_h = jnp.exp(-rate_h * 128.0)
    tail = jnp.concatenate([tail_h * half_h, tail_h], axis=2)
    whole_h = half_h * half_h
    whole = jnp.concatenate([whole_h, whole_h], axis=2)
    total = jnp.zeros(shape, jnp.float32)
    for b in range(nb):
        xb = x_ref[:, b * L:(b + 1) * L].astype(jnp.float32)
        total = total * whole + xb[None] * tail
    o_ref[...] = jnp.sum(total, axis=2)


def local_end_state(signal, params):
    rows, seg = signal.shape
    modes = params.shape[1]
    tc = 2 * tile_ch
    return pl.pallas_call(
        end_kernel,
        out_shape=jax.ShapeDtypeStruct((modes, rows), jnp.float32),
        grid=(rows // tc,),
        in_specs=[
            pl.BlockSpec((tc, seg), lambda i: (i, 0)),
            pl.BlockSpec((3, modes, tc), lambda i: (0, 0, i)),
        ],
        out_specs=pl.BlockSpec((modes, tc), lambda i: (0, i)),
        compiler_params=pltpu.CompilerParams(vmem_limit_bytes=48 * 1024 * 1024),
        cost_estimate=pl.CostEstimate(
            flops=3 * rows * seg * modes,
            transcendentals=2 * rows * block_len * modes,
            bytes_accessed=2 * rows * seg + 4 * modes * rows * 4,
        ),
    )(signal, params)


def per_device(residual_in, key_value, query_gate, decay_rates, residues, out_weight, norm_gain):
    rows, seg_len = key_value.shape
    n_seq = lax.axis_size("seq")
    total_len = n_seq * seg_len
    rates = decay_rates / total_len
    weights = residues * jnp.sqrt(2.0 * rates)
    zeros = jnp.zeros_like(rates.T)
    own_end = local_end_state(key_value, jnp.stack([rates.T, weights.T, zeros]))
    local = local_conv(key_value, jnp.stack([rates.T, weights.T, zeros]))
    me = lax.axis_index("seq")
    later = jnp.arange(n_seq)
    gap = jnp.maximum(later - 1 - me, 0).astype(jnp.float32) * seg_len
    reach = jnp.where(
        (later > me)[:, None, None], jnp.exp(-rates.T[None] * gap[:, None, None]), 0.0
    )
    sent = reach * own_end[None]
    received = lax.all_to_all(sent, "seq", 0, 0, tiled=True)
    carry_in = jnp.sum(received, axis=0)
    packed = jnp.stack([rates.T, weights.T, carry_in])
    gated = gated_conv(local, query_gate, packed)
    summed = lax.psum_scatter(
        lax.dot_general(
            out_weight, gated, (((0,), (0,)), ((), ())), preferred_element_type=jnp.float32
        ).astype(jnp.bfloat16),
        "ch",
        scatter_dimension=0,
        tiled=True,
    ).astype(jnp.float32)
    mixed = residual_in.astype(jnp.float32) + summed
    squares = jnp.sum(mixed * mixed, axis=0)
    n_ch = lax.axis_size("ch")
    partner = 1
    while partner < n_ch:
        squares = squares + lax.ppermute(squares, "ch", [(k, k ^ partner) for k in range(n_ch)])
        partner *= 2
    square_mean = squares / out_weight.shape[1]
    scaled = mixed * lax.rsqrt(square_mean + epsilon)[None, :] * norm_gain[:, None]
    return scaled.astype(jnp.bfloat16)


def solution(mesh):
    placed = (
        P("ch", "seq"),
        P("ch", "seq"),
        P("ch", "seq"),
        P("ch", None),
        P("ch", None),
        P("ch", None),
        P("ch"),
    )
    return jax.shard_map(
        per_device, mesh=mesh, in_specs=placed, out_specs=P("ch", "seq"), check_vma=False
    )
```
